256 devices in a mesh: face: 32 (over x, z), tile: 4 (over y), dp: 2 (over core).
Axes of the slice: x: 4, y: 4, z: 8, core: 2. Of those that a mesh axis runs over, the one named last changes fastest.
Arguments:
- loader: bfloat16 [2, 131072, 128], P('dp', ('face', 'tile')), may hold values from -6 to 6
- row_tile: int32 [131072], P(('face', 'tile')), may hold values from 0 to 127, as said below
- row_pixel: int32 [131072], P(('face', 'tile')), may hold values from 0 to 1023, as said below
- neighbours: int32 [128, 8], P(('face', 'tile')), may hold values from 0 to 128, as said below
- send_pixels: int32 [128, 8, 96], P(('face', 'tile')), may hold values from 0 to 1024, as said below
- halo_from: int32 [128, 420], P(('face', 'tile')), may hold values from 0 to 12288, as said below
- cotangent: bfloat16 [2, 131072, 128], P('dp', ('face', 'tile')), may hold values from -6 to 6
- kernel: bfloat16 [49, 128], replicated, may hold values from -0.875 to 0.875
- conv_bias: float32 [128], replicated, may hold values from -3 to 3
- norm_gain: float32 [128], replicated, may hold values from 0.1 to 1.9
- norm_bias: float32 [128], replicated, may hold values from -3 to 3
- weight_in: bfloat16 [128, 256], replicated, may hold values from -0.5 to 0.5
- bias_in: float32 [256], replicated, may hold values from -3 to 3
- weight_out: bfloat16 [256, 128], replicated, may hold values from -0.375 to 0.375
- bias_out: float32 [128], replicated, may hold values from -3 to 3
- layer_scale: float32 [128], replicated, may hold values from 0.3 to 1.5
Outputs:
- block_out: bfloat16 [2, 131072, 128], P('dp', ('face', 'tile'))
- field_grad: bfloat16 [2, 131072, 128], P('dp', ('face', 'tile'))
- grad_kernel: float32 [49, 128], replicated
- grad_conv_bias: float32 [128], replicated
- grad_norm_gain: float32 [128], replicated
- grad_norm_bias: float32 [128], replicated
- grad_weight_in: float32 [128, 256], replicated
- grad_bias_in: float32 [256], replicated
- grad_weight_out: float32 [256, 128], replicated
- grad_bias_out: float32 [128], replicated
- grad_layer_scale: float32 [128], replicated
The draws below stay inside these ranges and needn't reach their ends.
Inputs may be any that keep to these rules, and one draw needn't show every extreme that they name: Tile index = row * 4 + column on a grid of 32 x 4 tiles that wraps in both directions. neighbours[u, k] is either 128 (a missing link where only three tiles meet at a corner) or the tile at offset d_k from u, d_k the k-th of (-1,-1), (-1,0), (-1,1), (0,-1), (0,1), (1,-1), (1,0), (1,1) in (row, column). send_pixels[u, k] holds the pixels of tile u read by tile neighbours[u, k], in slot order; 1024 marks an unused slot. `halo_from`: each cycle cell of tile t names a slot of a link of the sending tile whose neighbours entry is t, or holds 128 * 96 (no source); one tile reads each slot at most once. `row_tile`: the 1024 loader rows of one device hold exactly 8 rows of each tile. Over all loader rows, (row_tile, row_pixel) takes each pixel of each tile exactly once.
All inputs are finite; a program needn't handle non-finite values.
Results may differ from the reference program's by a relative error of at most 0.0067.
Values may be sent and summed in bfloat16 or wider, within the bound.
No kernel may reach another device: no remote copies, remote signals or barrier semaphores. Data moves between devices by JAX's collectives and lax.ppermute only.
A program may use at most 64 MiB of HBM per device.

```python
import math
import jax
import jax.numpy as jnp
import numpy as np
from jax import lax

TILE_SIDE = 32
C = 128
HID = 256
GRID_ROWS = 32
GRID_COLS = 4
TILES = 128
BATCH = 2
PIX = 1024
CAP = 96
HALO = 420


def cycle_cells_drawn(tile_side):
    padded_side = tile_side + 6
    cell_rows, cell_cols = np.meshgrid(np.arange(padded_side), np.arange(padded_side), indexing='ij')
    inside = (cell_rows >= 3) & (cell_rows < tile_side + 3) & (cell_cols >= 3) & (cell_cols < tile_side + 3)
    outside = (~inside).reshape(-1)
    return (cell_rows.reshape(-1)[outside], cell_cols.reshape(-1)[outside])


def rotate(first, second, turns):
    out_first = jnp.where(turns == 0, first, jnp.where(turns == 1, -second, jnp.where(turns == 2, -first, second)))
    out_second = jnp.where(turns == 0, second, jnp.where(turns == 1, first, jnp.where(turns == 2, -second, -first)))
    return (out_first, out_second)


def geometry(key):
    tile_side = TILE_SIDE
    key_turn, key_vertex, key_force = jax.random.split(jax.random.fold_in(key, 11), 3)
    turning = jax.random.randint(key_turn, (TILES,), 0, 4).astype(jnp.int32)
    forced = jax.random.randint(key_force, (), 0, TILES)
    broken = (jax.random.randint(key_vertex, (TILES,), 0, 4) == 0) | (jnp.arange(TILES) == forced)
    cycle_rows, cycle_cols = cycle_cells_drawn(tile_side)
    local_row = jnp.asarray(cycle_rows - 3, jnp.int32)[None, :]
    local_col = jnp.asarray(cycle_cols - 3, jnp.int32)[None, :]
    cells = jnp.arange(TILES, dtype=jnp.int32)[:, None]
    grid_row = cells // GRID_COLS
    grid_col = cells % GRID_COLS
    rot_row, rot_col = rotate(2 * local_row - (tile_side - 1), 2 * local_col - (tile_side - 1), turning[:, None])
    glob_row = grid_row * tile_side + (tile_side - 1 + rot_row) // 2
    glob_col = grid_col * tile_side + (tile_side - 1 + rot_col) // 2
    owner_row = jnp.floor_divide(glob_row, tile_side)
    owner_col = jnp.floor_divide(glob_col, tile_side)
    step_row = owner_row - grid_row
    step_col = owner_col - grid_col
    source_cell = owner_row % GRID_ROWS * GRID_COLS + owner_col % GRID_COLS
    inner_row = glob_row - owner_row * tile_side
    inner_col = glob_col - owner_col * tile_side
    back_row, back_col = rotate(2 * inner_row - (tile_side - 1), 2 * inner_col - (tile_side - 1), (4 - turning[source_cell]) % 4)
    source_pixel = (back_row + tile_side - 1) // 2 * tile_side + (back_col + tile_side - 1) // 2
    course = (step_row + 1) * 3 + step_col + 1
    course = course - (course > 4).astype(jnp.int32)
    diagonal = (step_row != 0) & (step_col != 0)
    vertex = (grid_row + (step_row > 0).astype(jnp.int32)) % GRID_ROWS * GRID_COLS + (grid_col + (step_col > 0).astype(jnp.int32)) % GRID_COLS
    missing = diagonal & broken[vertex]
    onehot = (course[..., None] == jnp.arange(8, dtype=jnp.int32)).astype(jnp.int32)
    slot = jnp.sum(jnp.cumsum(onehot, axis=1) * onehot, axis=2) - 1
    receiver = jnp.broadcast_to(cells, course.shape)
    sender = source_cell
    opposite = 7 - course
    halo_from = jnp.where(missing, TILES * CAP, sender * CAP + slot).astype(jnp.int32)
    send_pixels = jnp.full((TILES, 8, CAP), PIX, jnp.int32).at[sender, opposite, slot].set(jnp.where(missing, PIX, source_pixel).astype(jnp.int32))
    neighbours = jnp.full((TILES, 8), TILES, jnp.int32).at[sender, opposite].set(jnp.where(missing, TILES, receiver).astype(jnp.int32))
    return (neighbours, send_pixels, halo_from)


def loader_map(key):
    per_peer = PIX // TILES
    key_pix, key_mix = jax.random.split(jax.random.fold_in(key, 23))

    def shuffle_one(subkey):
        return jax.random.permutation(subkey, PIX).astype(jnp.int32)
    pixel_orders = jax.vmap(shuffle_one)(jax.random.split(key_pix, TILES))
    slots = jnp.arange(PIX, dtype=jnp.int32)
    target_tile = slots // per_peer
    within = slots % per_peer
    devices = jnp.arange(TILES, dtype=jnp.int32)[:, None]
    base_pixel = pixel_orders[target_tile[None, :], devices * per_peer + within[None, :]]
    mixing = jax.vmap(shuffle_one)(jax.random.split(key_mix, TILES))
    tiles_out = jnp.take_along_axis(jnp.broadcast_to(target_tile[None, :], (TILES, PIX)), mixing, axis=1)
    pixels_out = jnp.take_along_axis(base_pixel, mixing, axis=1)
    return (tiles_out.reshape(-1), pixels_out.reshape(-1))


def draw_neighbours(key, part):
    return geometry(key)[0]


def draw_send_pixels(key, part):
    return geometry(key)[1]


def draw_halo_from(key, part):
    return geometry(key)[2]


def draw_row_tile(key, part):
    return loader_map(key)[0]


def draw_row_pixel(key, part):
    return loader_map(key)[1]


def level_of(stream_key, extent, pieces, smallest, high):
    factor_of = 1.0
    for dim, blocks in pieces:
        steps = jax.random.uniform(jax.random.fold_in(jax.random.fold_in(stream_key, 6), dim), (blocks,), jnp.float32, smallest / len(pieces), high / len(pieces))
        factor_of = factor_of * jnp.repeat(jnp.exp(steps), extent[dim] // blocks).reshape((-1,) + (1,) * (len(extent) - 1 - dim))
    return factor_of


def bell_draw(stream_key, extent, scale, bound, shards=(), held_as=jnp.bfloat16):
    drawn = jax.random.normal(stream_key, extent, jnp.float32) * scale
    if len(shards) > 0:
        drawn = level_of(stream_key, extent, shards, -0.22, 0.18) * drawn
    return jnp.clip(drawn, min=-bound, max=bound).astype(held_as)


def setup_inputs(seed: int = 0) -> dict:
    seeds = jax.random.split(jax.random.key(seed), 17)
    loader = bell_draw(seeds[0], (BATCH, TILES * PIX, C), 1.0, 6.0, ((0, 2), (1, 128)))
    row_tile = draw_row_tile(jax.random.fold_in(seeds[16], 71), 0)
    row_pixel = draw_row_pixel(jax.random.fold_in(seeds[16], 71), 0)
    neighbours = draw_neighbours(jax.random.fold_in(seeds[16], 71), 0)
    send_pixels = draw_send_pixels(jax.random.fold_in(seeds[16], 71), 0)
    halo_from = draw_halo_from(jax.random.fold_in(seeds[16], 71), 0)
    cotangent = bell_draw(seeds[6], (BATCH, TILES * PIX, C), 1.0, 6.0, ((0, 2), (1, 128)))
    kernel = bell_draw(seeds[7], (49, C), 49 ** -0.5, 0.875)
    conv_bias = bell_draw(seeds[8], (C,), 0.5, 3.0, (), jnp.float32)
    norm_gain = jnp.clip(1.0 + 0.18 * jax.random.normal(seeds[9], (C,), jnp.float32), 0.1, 1.9)
    norm_bias = bell_draw(seeds[10], (C,), 0.5, 3.0, (), jnp.float32)
    weight_in = bell_draw(seeds[11], (C, HID), C ** -0.5, 0.5)
    bias_in = bell_draw(seeds[12], (HID,), 0.5, 3.0, (), jnp.float32)
    weight_out = bell_draw(seeds[13], (HID, C), HID ** -0.5, 0.375)
    bias_out = bell_draw(seeds[14], (C,), 0.5, 3.0, (), jnp.float32)
    layer_scale = jnp.clip(jnp.exp(jax.random.uniform(seeds[15], (C,), jnp.float32, math.log(0.3), math.log(1.5))), 0.3, 1.5)
    return {"loader": loader, "row_tile": row_tile, "row_pixel": row_pixel, "neighbours": neighbours, "send_pixels": send_pixels, "halo_from": halo_from, "cotangent": cotangent, "kernel": kernel, "conv_bias": conv_bias, "norm_gain": norm_gain, "norm_bias": norm_bias, "weight_in": weight_in, "bias_in": bias_in, "weight_out": weight_out, "bias_out": bias_out, "layer_scale": layer_scale}


def cycle_cells(tile_side):
    padded_side = tile_side + 6
    cell_rows, cell_cols = np.meshgrid(np.arange(padded_side), np.arange(padded_side), indexing='ij')
    inside = (cell_rows >= 3) & (cell_rows < tile_side + 3) & (cell_cols >= 3) & (cell_cols < tile_side + 3)
    outside = (~inside).reshape(-1)
    return (cell_rows.reshape(-1)[outside], cell_cols.reshape(-1)[outside])

def depthwise(field_in, kern_in):
    return lax.conv_general_dilated(field_in, kern_in, (1, 1), 'VALID', dimension_numbers=('NHWC', 'HWIO', 'NHWC'), feature_group_count=field_in.shape[-1], precision=lax.Precision.HIGHEST)

def assemble(tile_rows, cycle_data):
    channels = tile_rows.shape[-1]
    tile_side = math.isqrt(tile_rows.shape[0])
    cycle_rows, cycle_cols = cycle_cells(tile_side)
    padded = jnp.zeros((tile_side + 6, tile_side + 6, channels), tile_rows.dtype)
    padded = padded.at[3:tile_side + 3, 3:tile_side + 3].set(tile_rows.reshape(tile_side, tile_side, channels))
    return padded.at[cycle_rows, cycle_cols].set(cycle_data)

def normal_cdf(values):
    return 0.5 * (1.0 + lax.erf(values * 0.7071067811865476))

def tile_pass(tile_rows, cycle_data, grad_rows, kernel, conv_bias, norm_gain, norm_bias, weight_in, bias_in, weight_out, bias_out, layer_scale):
    channels = tile_rows.shape[-1]
    pixel_count = tile_rows.shape[0]
    tile_side = math.isqrt(pixel_count)
    cycle_rows, cycle_cols = cycle_cells(tile_side)
    padded = assemble(tile_rows, cycle_data).astype(jnp.float32)[None]
    kern_f = kernel.astype(jnp.float32).reshape(7, 7, 1, channels)
    conv_out, conv_back = jax.vjp(depthwise, padded, kern_f)
    mixed = conv_out.reshape(pixel_count, channels) + conv_bias
    average = lax.optimization_barrier(jnp.mean(mixed, axis=-1, keepdims=True))
    centred = mixed - average
    inv_scale = lax.rsqrt(lax.optimization_barrier(jnp.mean(centred * centred, axis=-1, keepdims=True)) + 1e-06)
    standard = centred * inv_scale
    normed = (standard * norm_gain + norm_bias).astype(jnp.bfloat16)
    hidden = jnp.dot(normed, weight_in, preferred_element_type=jnp.float32) + bias_in
    cdf_vals = normal_cdf(hidden)
    active = (hidden * cdf_vals).astype(jnp.bfloat16)
    branch = jnp.dot(active, weight_out, preferred_element_type=jnp.float32) + bias_out
    output = (tile_rows.astype(jnp.float32) + layer_scale * branch).astype(jnp.bfloat16)
    grad_f = grad_rows.astype(jnp.float32)
    g_scale = lax.optimization_barrier(jnp.sum(grad_f * branch, axis=0))
    d_branch = (grad_f * layer_scale).astype(jnp.bfloat16)
    g_w_out = jnp.dot(active.T, d_branch, preferred_element_type=jnp.float32)
    g_b_out = lax.optimization_barrier(jnp.sum(d_branch.astype(jnp.float32), axis=0))
    d_active = jnp.dot(d_branch, weight_out.T, preferred_element_type=jnp.float32)
    slope = cdf_vals + hidden * jnp.exp(-0.5 * hidden * hidden) * 0.3989422804014327
    d_hidden = (d_active * slope).astype(jnp.bfloat16)
    g_w_in = jnp.dot(normed.T, d_hidden, preferred_element_type=jnp.float32)
    g_b_in = lax.optimization_barrier(jnp.sum(d_hidden.astype(jnp.float32), axis=0))
    d_normed = jnp.dot(d_hidden, weight_in.T, preferred_element_type=jnp.float32)
    g_gain = lax.optimization_barrier(jnp.sum(d_normed * standard, axis=0))
    g_nbias = lax.optimization_barrier(jnp.sum(d_normed, axis=0))
    scaled = d_normed * norm_gain
    d_mixed = (inv_scale * (scaled - lax.optimization_barrier(jnp.mean(scaled, axis=-1, keepdims=True)) - standard * lax.optimization_barrier(jnp.mean(scaled * standard, axis=-1, keepdims=True)))).astype(jnp.bfloat16)
    g_cbias = lax.optimization_barrier(jnp.sum(d_mixed.astype(jnp.float32), axis=0))
    d_pad, g_kern = conv_back(d_mixed.astype(jnp.float32).reshape(1, tile_side, tile_side, channels))
    d_pad = d_pad[0]
    inner_grad = d_pad[3:tile_side + 3, 3:tile_side + 3].reshape(pixel_count, channels)
    cycle_grad = d_pad[cycle_rows, cycle_cols].astype(jnp.bfloat16)
    partial_sums = (g_kern.reshape(49, channels), g_cbias, g_gain, g_nbias, g_w_in, g_b_in, g_w_out, g_b_out, g_scale)
    return (output, grad_f + inner_grad, cycle_grad, partial_sums)

def reference(loader, row_tile, row_pixel, neighbours, send_pixels, halo_from, cotangent, kernel, conv_bias, norm_gain, norm_bias, weight_in, bias_in, weight_out, bias_out, layer_scale):
    channels = loader.shape[-1]
    field = jnp.zeros_like(loader).at[:, row_tile * PIX + row_pixel].set(loader)
    blocks = field.reshape(BATCH, TILES, PIX, channels)
    extended = jnp.concatenate([blocks, jnp.zeros((BATCH, TILES, 1, channels), loader.dtype)], axis=2).reshape(BATCH, TILES * (PIX + 1), channels)
    sender = halo_from // CAP
    slot = halo_from % CAP
    clipped = jnp.minimum(sender, TILES - 1)
    receivers = jnp.arange(TILES, dtype=jnp.int32)[:, None, None]
    matches = neighbours[clipped] == receivers
    offers = send_pixels[clipped[..., None], jnp.arange(8, dtype=jnp.int32)[None, None, :], slot[..., None]]
    chosen = lax.optimization_barrier(jnp.sum(jnp.where(matches, offers, 0), axis=-1)).astype(jnp.int32)
    usable = jnp.any(matches, axis=-1) & (sender < TILES)
    source_pixel = jnp.where(usable, chosen, PIX).astype(jnp.int32)
    source_tile = jnp.where(usable, clipped, 0).astype(jnp.int32)
    flat_source = (source_tile * (PIX + 1) + source_pixel).astype(jnp.int32)
    cycles = extended[:, flat_source.reshape(-1)].reshape(BATCH * TILES, HALO, channels)
    grads = cotangent.reshape(BATCH * TILES, PIX, channels)

    def one_tile(item):
        return tile_pass(item[0], item[1], item[2], kernel, conv_bias, norm_gain, norm_bias, weight_in, bias_in, weight_out, bias_out, layer_scale)
    outputs, local_grads, cycle_grads, partial_sums = lax.map(one_tile, (blocks.reshape(BATCH * TILES, PIX, channels), cycles, grads))
    block_out = outputs.reshape(BATCH, TILES * PIX, channels)
    combined = jnp.concatenate([local_grads.reshape(BATCH, TILES, PIX, channels), jnp.zeros((BATCH, TILES, 1, channels), jnp.float32)], axis=2).reshape(BATCH, TILES * (PIX + 1), channels)
    combined = combined.at[:, flat_source.reshape(-1)].add(cycle_grads.reshape(BATCH, TILES * HALO, channels).astype(jnp.float32))
    field_grad = combined.reshape(BATCH, TILES, PIX + 1, channels)[:, :, :PIX].reshape(BATCH, TILES * PIX, channels).astype(jnp.bfloat16)
    factor = 1.0 / math.sqrt(BATCH * TILES * PIX)
    summed = [lax.optimization_barrier(jnp.sum(piece, axis=0)) * factor for piece in partial_sums]
    return (block_out, field_grad, summed[0], summed[1], summed[2], summed[3], summed[4], summed[5], summed[6], summed[7], summed[8])
```

```python
import math

import jax
import jax.numpy as jnp
import numpy as np
from jax import lax
from jax.sharding import PartitionSpec as P

LINK_OFFSETS = ((-1, -1), (-1, 0), (-1, 1), (0, -1), (0, 1), (1, -1), (1, 0), (1, 1))


def from_behind(value, axis, steps):
    count = lax.axis_size(axis)
    pairs = [(source, (source + steps) % count) for source in range(count)]
    return lax.ppermute(value, axis, pairs)


def tree_sum(parts, axes):
    flat = jnp.concatenate([part.reshape(-1) for part in parts])
    steps = []
    for axis in axes:
        size = lax.axis_size(axis)
        bit = 1
        while bit < size:
            steps.append((axis, bit, size))
            bit *= 2
    total = flat.shape[0]
    pad = (-total) % (1 << len(steps))
    buf = jnp.pad(flat, (0, pad))
    for axis, bit, size in steps:
        upper = (lax.axis_index(axis) // bit) % 2 == 1
        half = buf.shape[0] // 2
        low, high = buf[:half], buf[half:]
        keep = jnp.where(upper, high, low)
        send = jnp.where(upper, low, high)
        pairs = [(i, i ^ bit) for i in range(size)]
        buf = keep + lax.ppermute(send, axis, pairs)
    for axis, bit, size in reversed(steps):
        upper = (lax.axis_index(axis) // bit) % 2 == 1
        pairs = [(i, i ^ bit) for i in range(size)]
        got = lax.ppermute(buf, axis, pairs)
        buf = jnp.where(upper, jnp.concatenate([got, buf]), jnp.concatenate([buf, got]))
    out = []
    start = 0
    for part in parts:
        out.append(buf[start : start + part.size].reshape(part.shape))
        start += part.size
    return tuple(out)


def cycle_cells(tile_side):
    padded_side = tile_side + 6
    cell_rows, cell_cols = np.meshgrid(
        np.arange(padded_side), np.arange(padded_side), indexing="ij"
    )
    inside = (
        (cell_rows >= 3)
        & (cell_rows < tile_side + 3)
        & (cell_cols >= 3)
        & (cell_cols < tile_side + 3)
    )
    outside = (~inside).reshape(-1)
    return (cell_rows.reshape(-1)[outside], cell_cols.reshape(-1)[outside])


def depthwise(field_in, kern_in):
    return lax.conv_general_dilated(
        field_in,
        kern_in,
        (1, 1),
        "VALID",
        dimension_numbers=("NHWC", "HWIO", "NHWC"),
        feature_group_count=field_in.shape[-1],
        precision=lax.Precision.HIGHEST,
    )


def normal_cdf(values):
    return 0.5 * (1.0 + lax.erf(values * 0.7071067811865476))


def move_links(blocks, heading):
    pieces = []
    for link_index in range(8):
        row_step, col_step = LINK_OFFSETS[link_index]
        piece = blocks[link_index]
        if row_step != 0:
            piece = from_behind(piece, "face", heading * row_step)
        if col_step != 0:
            piece = from_behind(piece, "tile", heading * col_step)
        pieces.append(piece)
    return jnp.stack(pieces)


def local(
    loader,
    row_tile,
    row_pixel,
    neighbours,
    send_pixels,
    halo_from,
    cotangent,
    kernel,
    conv_bias,
    norm_gain,
    norm_bias,
    weight_in,
    bias_in,
    weight_out,
    bias_out,
    layer_scale,
):
    grid_rows = lax.axis_size("face")
    grid_cols = lax.axis_size("tile")
    tile_count = grid_rows * grid_cols
    pixel_count = loader.shape[1]
    channels = loader.shape[2]
    capacity = send_pixels.shape[2]
    per_peer = pixel_count // tile_count
    tile_side = math.isqrt(pixel_count)
    cycle_rows, cycle_cols = cycle_cells(tile_side)
    factor = 1.0 / math.sqrt(lax.axis_size("dp") * tile_count * pixel_count)
    ordering = jnp.argsort(row_tile, stable=True)
    outgoing = loader[0][ordering].reshape(tile_count, per_peer, channels)
    labels = row_pixel[ordering].reshape(tile_count, per_peer)
    arrived, places = (
        lax.all_to_all(outgoing, ("face", "tile"), split_axis=0, concat_axis=0, tiled=True),
        lax.all_to_all(labels, ("face", "tile"), split_axis=0, concat_axis=0, tiled=True),
    )
    field = (
        jnp.zeros((pixel_count, channels), loader.dtype)
        .at[places.reshape(-1)]
        .set(arrived.reshape(-1, channels))
    )
    my_row = lax.axis_index("face")
    my_col = lax.axis_index("tile")
    row_steps = jnp.asarray([offset[0] for offset in LINK_OFFSETS], jnp.int32)
    col_steps = jnp.asarray([offset[1] for offset in LINK_OFFSETS], jnp.int32)
    sources = (my_row - row_steps) % grid_rows * grid_cols + (my_col - col_steps) % grid_cols
    senders = halo_from[0] // capacity
    matching = senders[:, None] == sources[None, :]
    link_of = jnp.sum(matching.astype(jnp.int32) * jnp.arange(8, dtype=jnp.int32)[None, :], axis=1)
    readable = jnp.any(matching, axis=1)
    recv_index = jnp.where(readable, link_of * capacity + halo_from[0] % capacity, 8 * capacity)
    live = (neighbours[0] < tile_count)[:, None, None]
    extended = jnp.concatenate([field, jnp.zeros((1, channels), field.dtype)], axis=0)
    blocks_out = jnp.where(live, extended[send_pixels[0]], jnp.zeros((), field.dtype))
    received = move_links(blocks_out, 1)
    flat_recv = jnp.concatenate(
        [received.reshape(8 * capacity, channels), jnp.zeros((1, channels), field.dtype)], axis=0
    )
    cycle_data = flat_recv[recv_index]
    padded = jnp.zeros((tile_side + 6, tile_side + 6, channels), field.dtype)
    padded = padded.at[3 : tile_side + 3, 3 : tile_side + 3].set(
        field.reshape(tile_side, tile_side, channels)
    )
    padded = padded.at[cycle_rows, cycle_cols].set(cycle_data)
    kern_f = kernel.astype(jnp.float32).reshape(7, 7, 1, channels)
    conv_out, conv_back = jax.vjp(depthwise, padded.astype(jnp.float32)[None], kern_f)
    mixed = conv_out.reshape(pixel_count, channels) + conv_bias
    average = jnp.mean(mixed, axis=-1, keepdims=True)
    centred = mixed - average
    inv_scale = lax.rsqrt(jnp.mean(centred * centred, axis=-1, keepdims=True) + 1e-06)
    standard = centred * inv_scale
    normed = (standard * norm_gain + norm_bias).astype(jnp.bfloat16)
    hidden = jnp.dot(normed, weight_in, preferred_element_type=jnp.float32) + bias_in
    cdf_vals = normal_cdf(hidden)
    active = (hidden * cdf_vals).astype(jnp.bfloat16)
    branch = jnp.dot(active, weight_out, preferred_element_type=jnp.float32) + bias_out
    block_out = (field.astype(jnp.float32) + layer_scale * branch).astype(jnp.bfloat16)
    grad_f = cotangent[0].astype(jnp.float32)
    g_scale = jnp.sum(grad_f * branch, axis=0) * factor
    d_branch = (grad_f * layer_scale).astype(jnp.bfloat16)
    g_w_out = jnp.dot(active.T, d_branch, preferred_element_type=jnp.float32) * factor
    g_b_out = jnp.sum(d_branch.astype(jnp.float32), axis=0) * factor
    d_active = jnp.dot(d_branch, weight_out.T, preferred_element_type=jnp.float32)
    slope = cdf_vals + hidden * jnp.exp(-0.5 * hidden * hidden) * 0.3989422804014327
    d_hidden = (d_active * slope).astype(jnp.bfloat16)
    g_w_in = jnp.dot(normed.T, d_hidden, preferred_element_type=jnp.float32) * factor
    g_b_in = jnp.sum(d_hidden.astype(jnp.float32), axis=0) * factor
    d_normed = jnp.dot(d_hidden, weight_in.T, preferred_element_type=jnp.float32)
    g_gain = jnp.sum(d_normed * standard, axis=0) * factor
    g_nbias = jnp.sum(d_normed, axis=0) * factor
    scaled = d_normed * norm_gain
    d_mixed = (
        inv_scale
        * (
            scaled
            - jnp.mean(scaled, axis=-1, keepdims=True)
            - standard * jnp.mean(scaled * standard, axis=-1, keepdims=True)
        )
    ).astype(jnp.bfloat16)
    g_cbias = jnp.sum(d_mixed.astype(jnp.float32), axis=0) * factor
    d_pad, g_kern = conv_back(
        d_mixed.astype(jnp.float32).reshape(1, tile_side, tile_side, channels)
    )
    d_pad = d_pad[0]
    g_kern = g_kern.reshape(49, channels) * factor
    inner_grad = d_pad[3 : tile_side + 3, 3 : tile_side + 3].reshape(pixel_count, channels)
    cycle_grad = d_pad[cycle_rows, cycle_cols].astype(jnp.bfloat16)
    back_parcel = (
        jnp.zeros((8 * capacity + 1, channels), jnp.bfloat16).at[recv_index].set(cycle_grad)
    )
    back_parcel = back_parcel[: 8 * capacity].reshape(8, capacity, channels)
    returned = move_links(back_parcel, -1)
    returned = jnp.where(live, returned, jnp.zeros((), returned.dtype))
    incoming = (
        jnp.zeros((pixel_count + 1, channels), jnp.float32)
        .at[send_pixels[0].reshape(-1)]
        .add(returned.reshape(-1, channels).astype(jnp.float32))
    )
    field_grad = (grad_f + inner_grad + incoming[:pixel_count]).astype(jnp.bfloat16)
    g_kern, g_cbias, g_gain, g_nbias, g_w_in, g_b_in, g_w_out, g_b_out, g_scale = tree_sum(
        (g_kern, g_cbias, g_gain, g_nbias, g_w_in, g_b_in, g_w_out, g_b_out, g_scale),
        ("dp", "tile", "face"),
    )
    return (
        block_out[None],
        field_grad[None],
        g_kern,
        g_cbias,
        g_gain,
        g_nbias,
        g_w_in,
        g_b_in,
        g_w_out,
        g_b_out,
        g_scale,
    )


def solution(mesh):
    placed = (
        P("dp", ("face", "tile"), None),
        P(("face", "tile")),
        P(("face", "tile")),
        P(("face", "tile"), None),
        P(("face", "tile"), None, None),
        P(("face", "tile"), None),
        P("dp", ("face", "tile"), None),
        P(),
        P(),
        P(),
        P(),
        P(),
        P(),
        P(),
        P(),
        P(),
    )
    return jax.shard_map(
        local,
        mesh=mesh,
        in_specs=placed,
        out_specs=(
            P("dp", ("face", "tile"), None),
            P("dp", ("face", "tile"), None),
            P(),
            P(),
            P(),
            P(),
            P(),
            P(),
            P(),
            P(),
            P(),
        ),
        check_vma=False,
    )
```

```python
import math

import jax
import jax.numpy as jnp
import numpy as np
from jax import lax
from jax.sharding import PartitionSpec as P

LINK_OFFSETS = ((-1, -1), (-1, 0), (-1, 1), (0, -1), (0, 1), (1, -1), (1, 0), (1, 1))


def from_behind(value, axis, steps):
    count = lax.axis_size(axis)
    pairs = [(source, (source + steps) % count) for source in range(count)]
    return lax.ppermute(value, axis, pairs)


def tree_sum(parts, axes):
    flat = jnp.concatenate([part.reshape(-1) for part in parts])
    steps = []
    for axis in axes:
        size = lax.axis_size(axis)
        bit = 1
        while bit < size:
            steps.append((axis, bit, size))
            bit *= 2
    total = flat.shape[0]
    pad = (-total) % (1 << len(steps))
    buf = jnp.pad(flat, (0, pad))
    for axis, bit, size in steps:
        upper = (lax.axis_index(axis) // bit) % 2 == 1
        half = buf.shape[0] // 2
        low, high = buf[:half], buf[half:]
        keep = jnp.where(upper, high, low)
        send = jnp.where(upper, low, high)
        pairs = [(i, i ^ bit) for i in range(size)]
        buf = keep + lax.ppermute(send, axis, pairs)
    for axis, bit, size in reversed(steps):
        upper = (lax.axis_index(axis) // bit) % 2 == 1
        pairs = [(i, i ^ bit) for i in range(size)]
        got = lax.ppermute(buf, axis, pairs)
        buf = jnp.where(upper, jnp.concatenate([got, buf]), jnp.concatenate([buf, got]))
    out = []
    start = 0
    for part in parts:
        out.append(buf[start : start + part.size].reshape(part.shape))
        start += part.size
    return tuple(out)


def cycle_cells(tile_side):
    padded_side = tile_side + 6
    cell_rows, cell_cols = np.meshgrid(
        np.arange(padded_side), np.arange(padded_side), indexing="ij"
    )
    inside = (
        (cell_rows >= 3)
        & (cell_rows < tile_side + 3)
        & (cell_cols >= 3)
        & (cell_cols < tile_side + 3)
    )
    outside = (~inside).reshape(-1)
    return (cell_rows.reshape(-1)[outside], cell_cols.reshape(-1)[outside])


def depthwise(field_in, kern_in):
    return lax.conv_general_dilated(
        field_in,
        kern_in,
        (1, 1),
        "VALID",
        dimension_numbers=("NHWC", "HWIO", "NHWC"),
        feature_group_count=field_in.shape[-1],
        precision=lax.Precision.HIGHEST,
    )


def assemble(tile, cycle_data):
    side = tile.shape[0]
    wide = side + 6
    channels = tile.shape[-1]
    band = 3 * wide
    top = cycle_data[:band].reshape(3, wide, channels)
    middle = cycle_data[band : band + 6 * side].reshape(side, 6, channels)
    bottom = cycle_data[band + 6 * side :].reshape(3, wide, channels)
    centre = jnp.concatenate([middle[:, :3], tile, middle[:, 3:]], axis=1)
    return jnp.concatenate([top, centre, bottom], axis=0)


def ring_of(square, side):
    channels = square.shape[-1]
    top = square[:3].reshape(-1, channels)
    middle = jnp.concatenate([square[3 : side + 3, :3], square[3 : side + 3, side + 3 :]], axis=1)
    bottom = square[side + 3 :].reshape(-1, channels)
    return jnp.concatenate([top, middle.reshape(-1, channels), bottom], axis=0)


def normal_cdf(values):
    return 0.5 * (1.0 + lax.erf(values * 0.7071067811865476))


def move_links(blocks, heading):
    ups = [k for k, offset in enumerate(LINK_OFFSETS) if offset[0] == -1]
    downs = [k for k, offset in enumerate(LINK_OFFSETS) if offset[0] == 1]
    moved = list(blocks[k] for k in range(len(LINK_OFFSETS)))
    for group, step in ((ups, -heading), (downs, heading)):
        shifted = from_behind(jnp.stack([moved[k] for k in group]), "face", step)
        for place, k in enumerate(group):
            moved[k] = shifted[place]
    lefts = [k for k, offset in enumerate(LINK_OFFSETS) if offset[1] == -1]
    rights = [k for k, offset in enumerate(LINK_OFFSETS) if offset[1] == 1]
    for group, step in ((lefts, -heading), (rights, heading)):
        shifted = from_behind(jnp.stack([moved[k] for k in group]), "tile", step)
        for place, k in enumerate(group):
            moved[k] = shifted[place]
    return jnp.stack(moved)


def local(
    loader,
    row_tile,
    row_pixel,
    neighbours,
    send_pixels,
    halo_from,
    cotangent,
    kernel,
    conv_bias,
    norm_gain,
    norm_bias,
    weight_in,
    bias_in,
    weight_out,
    bias_out,
    layer_scale,
):
    grid_rows = lax.axis_size("face")
    grid_cols = lax.axis_size("tile")
    tile_count = grid_rows * grid_cols
    pixel_count = loader.shape[1]
    channels = loader.shape[2]
    capacity = send_pixels.shape[2]
    per_peer = pixel_count // tile_count
    tile_side = math.isqrt(pixel_count)
    cycle_rows, cycle_cols = cycle_cells(tile_side)
    factor = 1.0 / math.sqrt(lax.axis_size("dp") * tile_count * pixel_count)
    ordering = jnp.argsort(row_tile, stable=True)
    outgoing = loader[0][ordering].reshape(tile_count, per_peer, channels)
    labels = row_pixel[ordering].reshape(tile_count, per_peer)
    digits = jnp.concatenate([labels // 32, labels % 32], axis=1).astype(loader.dtype)
    label_row = jnp.pad(digits, ((0, 0), (0, channels - 2 * per_peer)))[:, None, :]
    parcel = lax.all_to_all(
        jnp.concatenate([outgoing, label_row], axis=1),
        ("face", "tile"),
        split_axis=0,
        concat_axis=0,
        tiled=True,
    )
    arrived = parcel[:, :per_peer]
    got = parcel[:, per_peer, : 2 * per_peer].astype(jnp.int32)
    places = got[:, :per_peer] * 32 + got[:, per_peer:]
    field = (
        jnp.zeros((pixel_count, channels), loader.dtype)
        .at[places.reshape(-1)]
        .set(arrived.reshape(-1, channels))
    )
    my_row = lax.axis_index("face")
    my_col = lax.axis_index("tile")
    row_steps = jnp.asarray([offset[0] for offset in LINK_OFFSETS], jnp.int32)
    col_steps = jnp.asarray([offset[1] for offset in LINK_OFFSETS], jnp.int32)
    sources = (my_row - row_steps) % grid_rows * grid_cols + (my_col - col_steps) % grid_cols
    senders = halo_from[0] // capacity
    matching = senders[:, None] == sources[None, :]
    link_of = jnp.sum(matching.astype(jnp.int32) * jnp.arange(8, dtype=jnp.int32)[None, :], axis=1)
    readable = jnp.any(matching, axis=1)
    recv_index = jnp.where(readable, link_of * capacity + halo_from[0] % capacity, 8 * capacity)
    live = (neighbours[0] < tile_count)[:, None, None]
    extended = jnp.concatenate([field, jnp.zeros((1, channels), field.dtype)], axis=0)
    blocks_out = jnp.where(live, extended[send_pixels[0]], jnp.zeros((), field.dtype))
    received = move_links(blocks_out, 1)
    flat_recv = jnp.concatenate(
        [received.reshape(8 * capacity, channels), jnp.zeros((1, channels), field.dtype)], axis=0
    )
    cycle_data = flat_recv[recv_index]
    padded = assemble(field.reshape(tile_side, tile_side, channels), cycle_data)
    kern_f = kernel.astype(jnp.float32).reshape(7, 7, 1, channels)
    conv_out, conv_back = jax.vjp(depthwise, padded.astype(jnp.float32)[None], kern_f)
    mixed = conv_out.reshape(pixel_count, channels) + conv_bias
    average = jnp.mean(mixed, axis=-1, keepdims=True)
    centred = mixed - average
    inv_scale = lax.rsqrt(jnp.mean(centred * centred, axis=-1, keepdims=True) + 1e-06)
    standard = centred * inv_scale
    normed = (standard * norm_gain + norm_bias).astype(jnp.bfloat16)
    hidden = jnp.dot(normed, weight_in, preferred_element_type=jnp.float32) + bias_in
    cdf_vals = normal_cdf(hidden)
    active = (hidden * cdf_vals).astype(jnp.bfloat16)
    branch = jnp.dot(active, weight_out, preferred_element_type=jnp.float32) + bias_out
    block_out = (field.astype(jnp.float32) + layer_scale * branch).astype(jnp.bfloat16)
    grad_f = cotangent[0].astype(jnp.float32)
    g_scale = jnp.sum(grad_f * branch, axis=0) * factor
    d_branch = (grad_f * layer_scale).astype(jnp.bfloat16)
    g_w_out = jnp.dot(active.T, d_branch, preferred_element_type=jnp.float32) * factor
    g_b_out = jnp.sum(d_branch.astype(jnp.float32), axis=0) * factor
    d_active = jnp.dot(d_branch, weight_out.T, preferred_element_type=jnp.float32)
    slope = cdf_vals + hidden * jnp.exp(-0.5 * hidden * hidden) * 0.3989422804014327
    d_hidden = (d_active * slope).astype(jnp.bfloat16)
    g_w_in = jnp.dot(normed.T, d_hidden, preferred_element_type=jnp.float32) * factor
    g_b_in = jnp.sum(d_hidden.astype(jnp.float32), axis=0) * factor
    d_normed = jnp.dot(d_hidden, weight_in.T, preferred_element_type=jnp.float32)
    g_gain = jnp.sum(d_normed * standard, axis=0) * factor
    g_nbias = jnp.sum(d_normed, axis=0) * factor
    scaled = d_normed * norm_gain
    d_mixed = (
        inv_scale
        * (
            scaled
            - jnp.mean(scaled, axis=-1, keepdims=True)
            - standard * jnp.mean(scaled * standard, axis=-1, keepdims=True)
        )
    ).astype(jnp.bfloat16)
    g_cbias = jnp.sum(d_mixed.astype(jnp.float32), axis=0) * factor
    d_pad, g_kern = conv_back(
        d_mixed.astype(jnp.float32).reshape(1, tile_side, tile_side, channels)
    )
    d_pad = d_pad[0]
    g_kern = g_kern.reshape(49, channels) * factor
    inner_grad = d_pad[3 : tile_side + 3, 3 : tile_side + 3].reshape(pixel_count, channels)
    cycle_grad = ring_of(d_pad, tile_side).astype(jnp.bfloat16)
    back_parcel = (
        jnp.zeros((8 * capacity + 1, channels), jnp.bfloat16).at[recv_index].set(cycle_grad)
    )
    back_parcel = back_parcel[: 8 * capacity].reshape(8, capacity, channels)
    returned = move_links(back_parcel, -1)
    returned = jnp.where(live, returned, jnp.zeros((), returned.dtype))
    incoming = (
        jnp.zeros((pixel_count + 1, channels), jnp.float32)
        .at[send_pixels[0].reshape(-1)]
        .add(returned.reshape(-1, channels).astype(jnp.float32))
    )
    field_grad = (grad_f + inner_grad + incoming[:pixel_count]).astype(jnp.bfloat16)
    g_kern, g_cbias, g_gain, g_nbias, g_w_in, g_b_in, g_w_out, g_b_out, g_scale = tree_sum(
        (g_kern, g_cbias, g_gain, g_nbias, g_w_in, g_b_in, g_w_out, g_b_out, g_scale),
        ("dp", "tile", "face"),
    )
    return (
        block_out[None],
        field_grad[None],
        g_kern,
        g_cbias,
        g_gain,
        g_nbias,
        g_w_in,
        g_b_in,
        g_w_out,
        g_b_out,
        g_scale,
    )


def solution(mesh):
    placed = (
        P("dp", ("face", "tile"), None),
        P(("face", "tile")),
        P(("face", "tile")),
        P(("face", "tile"), None),
        P(("face", "tile"), None, None),
        P(("face", "tile"), None),
        P("dp", ("face", "tile"), None),
        P(),
        P(),
        P(),
        P(),
        P(),
        P(),
        P(),
        P(),
        P(),
    )
    return jax.shard_map(
        local,
        mesh=mesh,
        in_specs=placed,
        out_specs=(
            P("dp", ("face", "tile"), None),
            P("dp", ("face", "tile"), None),
            P(),
            P(),
            P(),
            P(),
            P(),
            P(),
            P(),
            P(),
            P(),
        ),
        check_vma=False,
    )
```

```python
import math

import jax
import jax.numpy as jnp
import numpy as np
from jax import lax
from jax.sharding import PartitionSpec as P

LINK_OFFSETS = ((-1, -1), (-1, 0), (-1, 1), (0, -1), (0, 1), (1, -1), (1, 0), (1, 1))


def from_behind(value, axis, steps):
    count = lax.axis_size(axis)
    pairs = [(source, (source + steps) % count) for source in range(count)]
    return lax.ppermute(value, axis, pairs)


def tree_sum(parts, axes):
    flat = jnp.concatenate([part.reshape(-1) for part in parts])
    steps = []
    for axis in axes:
        size = lax.axis_size(axis)
        bit = 1
        while bit < size:
            steps.append((axis, bit, size))
            bit *= 2
    total = flat.shape[0]
    pad = (-total) % (1 << len(steps))
    buf = jnp.pad(flat, (0, pad))
    for axis, bit, size in steps:
        upper = (lax.axis_index(axis) // bit) % 2 == 1
        half = buf.shape[0] // 2
        low, high = buf[:half], buf[half:]
        keep = jnp.where(upper, high, low)
        send = jnp.where(upper, low, high)
        pairs = [(i, i ^ bit) for i in range(size)]
        buf = keep + lax.ppermute(send, axis, pairs)
    for axis, bit, size in reversed(steps):
        upper = (lax.axis_index(axis) // bit) % 2 == 1
        pairs = [(i, i ^ bit) for i in range(size)]
        got = lax.ppermute(buf, axis, pairs)
        buf = jnp.where(upper, jnp.concatenate([got, buf]), jnp.concatenate([buf, got]))
    out = []
    start = 0
    for part in parts:
        out.append(buf[start : start + part.size].reshape(part.shape))
        start += part.size
    return tuple(out)


def doubling_sum(parts, axes):
    flat = jnp.concatenate([part.reshape(-1) for part in parts])
    for axis in axes:
        size = lax.axis_size(axis)
        bit = 1
        while bit < size:
            flat = flat + lax.ppermute(flat, axis, [(i, i ^ bit) for i in range(size)])
            bit *= 2
    out = []
    start = 0
    for part in parts:
        out.append(flat[start : start + part.size].reshape(part.shape))
        start += part.size
    return tuple(out)


def cycle_cells(tile_side):
    padded_side = tile_side + 6
    cell_rows, cell_cols = np.meshgrid(
        np.arange(padded_side), np.arange(padded_side), indexing="ij"
    )
    inside = (
        (cell_rows >= 3)
        & (cell_rows < tile_side + 3)
        & (cell_cols >= 3)
        & (cell_cols < tile_side + 3)
    )
    outside = (~inside).reshape(-1)
    return (cell_rows.reshape(-1)[outside], cell_cols.reshape(-1)[outside])


def depthwise(field_in, kern_in):
    return lax.conv_general_dilated(
        field_in,
        kern_in,
        (1, 1),
        "VALID",
        dimension_numbers=("NHWC", "HWIO", "NHWC"),
        feature_group_count=field_in.shape[-1],
        precision=lax.Precision.HIGHEST,
    )


def assemble(tile, cycle_data):
    side = tile.shape[0]
    wide = side + 6
    channels = tile.shape[-1]
    band = 3 * wide
    top = cycle_data[:band].reshape(3, wide, channels)
    middle = cycle_data[band : band + 6 * side].reshape(side, 6, channels)
    bottom = cycle_data[band + 6 * side :].reshape(3, wide, channels)
    centre = jnp.concatenate([middle[:, :3], tile, middle[:, 3:]], axis=1)
    return jnp.concatenate([top, centre, bottom], axis=0)


def ring_of(square, side):
    channels = square.shape[-1]
    top = square[:3].reshape(-1, channels)
    middle = jnp.concatenate([square[3 : side + 3, :3], square[3 : side + 3, side + 3 :]], axis=1)
    bottom = square[side + 3 :].reshape(-1, channels)
    return jnp.concatenate([top, middle.reshape(-1, channels), bottom], axis=0)


def normal_cdf(values):
    return 0.5 * (1.0 + lax.erf(values * 0.7071067811865476))


def move_links(blocks, heading):
    ups = [k for k, offset in enumerate(LINK_OFFSETS) if offset[0] == -1]
    downs = [k for k, offset in enumerate(LINK_OFFSETS) if offset[0] == 1]
    moved = list(blocks[k] for k in range(len(LINK_OFFSETS)))
    for group, step in ((ups, -heading), (downs, heading)):
        shifted = from_behind(jnp.stack([moved[k] for k in group]), "face", step)
        for place, k in enumerate(group):
            moved[k] = shifted[place]
    lefts = [k for k, offset in enumerate(LINK_OFFSETS) if offset[1] == -1]
    rights = [k for k, offset in enumerate(LINK_OFFSETS) if offset[1] == 1]
    for group, step in ((lefts, -heading), (rights, heading)):
        shifted = from_behind(jnp.stack([moved[k] for k in group]), "tile", step)
        for place, k in enumerate(group):
            moved[k] = shifted[place]
    return jnp.stack(moved)


def local(
    loader,
    row_tile,
    row_pixel,
    neighbours,
    send_pixels,
    halo_from,
    cotangent,
    kernel,
    conv_bias,
    norm_gain,
    norm_bias,
    weight_in,
    bias_in,
    weight_out,
    bias_out,
    layer_scale,
):
    grid_rows = lax.axis_size("face")
    grid_cols = lax.axis_size("tile")
    tile_count = grid_rows * grid_cols
    pixel_count = loader.shape[1]
    channels = loader.shape[2]
    capacity = send_pixels.shape[2]
    per_peer = pixel_count // tile_count
    tile_side = math.isqrt(pixel_count)
    cycle_rows, cycle_cols = cycle_cells(tile_side)
    factor = 1.0 / math.sqrt(lax.axis_size("dp") * tile_count * pixel_count)
    ordering = jnp.argsort(row_tile, stable=True)
    outgoing = loader[0][ordering].reshape(tile_count, per_peer, channels)
    labels = row_pixel[ordering].reshape(tile_count, per_peer)
    digits = jnp.concatenate([labels // 32, labels % 32], axis=1).astype(loader.dtype)
    label_row = jnp.pad(digits, ((0, 0), (0, channels - 2 * per_peer)))[:, None, :]
    parcel = lax.all_to_all(
        jnp.concatenate([outgoing, label_row], axis=1),
        ("face", "tile"),
        split_axis=0,
        concat_axis=0,
        tiled=True,
    )
    arrived = parcel[:, :per_peer]
    got = parcel[:, per_peer, : 2 * per_peer].astype(jnp.int32)
    places = got[:, :per_peer] * 32 + got[:, per_peer:]
    field = (
        jnp.zeros((pixel_count, channels), loader.dtype)
        .at[places.reshape(-1)]
        .set(arrived.reshape(-1, channels))
    )
    my_row = lax.axis_index("face")
    my_col = lax.axis_index("tile")
    row_steps = jnp.asarray([offset[0] for offset in LINK_OFFSETS], jnp.int32)
    col_steps = jnp.asarray([offset[1] for offset in LINK_OFFSETS], jnp.int32)
    sources = (my_row - row_steps) % grid_rows * grid_cols + (my_col - col_steps) % grid_cols
    senders = halo_from[0] // capacity
    matching = senders[:, None] == sources[None, :]
    link_of = jnp.sum(matching.astype(jnp.int32) * jnp.arange(8, dtype=jnp.int32)[None, :], axis=1)
    readable = jnp.any(matching, axis=1)
    recv_index = jnp.where(readable, link_of * capacity + halo_from[0] % capacity, 8 * capacity)
    live = (neighbours[0] < tile_count)[:, None, None]
    extended = jnp.concatenate([field, jnp.zeros((1, channels), field.dtype)], axis=0)
    blocks_out = jnp.where(live, extended[send_pixels[0]], jnp.zeros((), field.dtype))
    received = move_links(blocks_out, 1)
    flat_recv = jnp.concatenate(
        [received.reshape(8 * capacity, channels), jnp.zeros((1, channels), field.dtype)], axis=0
    )
    cycle_data = flat_recv[recv_index]
    padded = assemble(field.reshape(tile_side, tile_side, channels), cycle_data)
    kern_f = kernel.astype(jnp.float32).reshape(7, 7, 1, channels)
    conv_out, conv_back = jax.vjp(depthwise, padded.astype(jnp.float32)[None], kern_f)
    mixed = conv_out.reshape(pixel_count, channels) + conv_bias
    average = jnp.mean(mixed, axis=-1, keepdims=True)
    centred = mixed - average
    inv_scale = lax.rsqrt(jnp.mean(centred * centred, axis=-1, keepdims=True) + 1e-06)
    standard = centred * inv_scale
    normed = (standard * norm_gain + norm_bias).astype(jnp.bfloat16)
    hidden = jnp.dot(normed, weight_in, preferred_element_type=jnp.float32) + bias_in
    cdf_vals = normal_cdf(hidden)
    active = (hidden * cdf_vals).astype(jnp.bfloat16)
    branch = jnp.dot(active, weight_out, preferred_element_type=jnp.float32) + bias_out
    block_out = (field.astype(jnp.float32) + layer_scale * branch).astype(jnp.bfloat16)
    grad_f = cotangent[0].astype(jnp.float32)
    g_scale = jnp.sum(grad_f * branch, axis=0) * factor
    d_branch = (grad_f * layer_scale).astype(jnp.bfloat16)
    g_w_out = jnp.dot(active.T, d_branch, preferred_element_type=jnp.float32) * factor
    g_b_out = jnp.sum(d_branch.astype(jnp.float32), axis=0) * factor
    d_active = jnp.dot(d_branch, weight_out.T, preferred_element_type=jnp.float32)
    slope = cdf_vals + hidden * jnp.exp(-0.5 * hidden * hidden) * 0.3989422804014327
    d_hidden = (d_active * slope).astype(jnp.bfloat16)
    g_w_in = jnp.dot(normed.T, d_hidden, preferred_element_type=jnp.float32) * factor
    g_b_in = jnp.sum(d_hidden.astype(jnp.float32), axis=0) * factor
    d_normed = jnp.dot(d_hidden, weight_in.T, preferred_element_type=jnp.float32)
    g_gain = jnp.sum(d_normed * standard, axis=0) * factor
    g_nbias = jnp.sum(d_normed, axis=0) * factor
    g_gain, g_nbias, g_w_in, g_b_in, g_w_out, g_b_out, g_scale = tree_sum(
        (g_gain, g_nbias, g_w_in, g_b_in, g_w_out, g_b_out, g_scale), ("dp", "tile", "face")
    )
    scaled = d_normed * norm_gain
    d_mixed = (
        inv_scale
        * (
            scaled
            - jnp.mean(scaled, axis=-1, keepdims=True)
            - standard * jnp.mean(scaled * standard, axis=-1, keepdims=True)
        )
    ).astype(jnp.bfloat16)
    g_cbias = jnp.sum(d_mixed.astype(jnp.float32), axis=0) * factor
    d_pad, g_kern = conv_back(
        d_mixed.astype(jnp.float32).reshape(1, tile_side, tile_side, channels)
    )
    d_pad = d_pad[0]
    g_kern = g_kern.reshape(49, channels) * factor
    inner_grad = d_pad[3 : tile_side + 3, 3 : tile_side + 3].reshape(pixel_count, channels)
    cycle_grad = ring_of(d_pad, tile_side).astype(jnp.bfloat16)
    back_parcel = (
        jnp.zeros((8 * capacity + 1, channels), jnp.bfloat16).at[recv_index].set(cycle_grad)
    )
    back_parcel = back_parcel[: 8 * capacity].reshape(8, capacity, channels)
    returned = move_links(back_parcel, -1)
    returned = jnp.where(live, returned, jnp.zeros((), returned.dtype))
    incoming = (
        jnp.zeros((pixel_count + 1, channels), jnp.float32)
        .at[send_pixels[0].reshape(-1)]
        .add(returned.reshape(-1, channels).astype(jnp.float32))
    )
    field_grad = (grad_f + inner_grad + incoming[:pixel_count]).astype(jnp.bfloat16)
    g_kern, g_cbias = doubling_sum((g_kern, g_cbias), ("dp", "tile", "face"))
    return (
        block_out[None],
        field_grad[None],
        g_kern,
        g_cbias,
        g_gain,
        g_nbias,
        g_w_in,
        g_b_in,
        g_w_out,
        g_b_out,
        g_scale,
    )


def solution(mesh):
    placed = (
        P("dp", ("face", "tile"), None),
        P(("face", "tile")),
        P(("face", "tile")),
        P(("face", "tile"), None),
        P(("face", "tile"), None, None),
        P(("face", "tile"), None),
        P("dp", ("face", "tile"), None),
        P(),
        P(),
        P(),
        P(),
        P(),
        P(),
        P(),
        P(),
        P(),
    )
    return jax.shard_map(
        local,
        mesh=mesh,
        in_specs=placed,
        out_specs=(
            P("dp", ("face", "tile"), None),
            P("dp", ("face", "tile"), None),
            P(),
            P(),
            P(),
            P(),
            P(),
            P(),
            P(),
            P(),
            P(),
        ),
        check_vma=False,
    )
```

```python
import math

import jax
import jax.numpy as jnp
import numpy as np
from jax import lax
from jax.sharding import PartitionSpec as P

LINK_OFFSETS = ((-1, -1), (-1, 0), (-1, 1), (0, -1), (0, 1), (1, -1), (1, 0), (1, 1))


def from_behind(value, axis, steps):
    count = lax.axis_size(axis)
    pairs = [(source, (source + steps) % count) for source in range(count)]
    return lax.ppermute(value, axis, pairs)


def tree_sum(parts, halving_axes, doubling_axes):
    flat = jnp.concatenate([part.reshape(-1) for part in parts])

    def bits_of(axes):
        steps = []
        for axis in axes:
            size = lax.axis_size(axis)
            bit = 1
            while bit < size:
                steps.append((axis, bit, size))
                bit *= 2
        return steps

    halving = bits_of(halving_axes)
    total = flat.shape[0]
    pad = (-total) % (1 << len(halving))
    buf = jnp.pad(flat, (0, pad))
    for axis, bit, size in halving:
        upper = (lax.axis_index(axis) // bit) % 2 == 1
        half = buf.shape[0] // 2
        low, high = buf[:half], buf[half:]
        keep = jnp.where(upper, high, low)
        send = jnp.where(upper, low, high)
        pairs = [(i, i ^ bit) for i in range(size)]
        buf = keep + lax.ppermute(send, axis, pairs)
    for axis, bit, size in bits_of(doubling_axes):
        buf = buf + lax.ppermute(buf, axis, [(i, i ^ bit) for i in range(size)])
    for axis, bit, size in reversed(halving):
        upper = (lax.axis_index(axis) // bit) % 2 == 1
        pairs = [(i, i ^ bit) for i in range(size)]
        got = lax.ppermute(buf, axis, pairs)
        buf = jnp.where(upper, jnp.concatenate([got, buf]), jnp.concatenate([buf, got]))
    out = []
    start = 0
    for part in parts:
        out.append(buf[start : start + part.size].reshape(part.shape))
        start += part.size
    return tuple(out)

def cycle_cells(tile_side):
    padded_side = tile_side + 6
    cell_rows, cell_cols = np.meshgrid(
        np.arange(padded_side), np.arange(padded_side), indexing="ij"
    )
    inside = (
        (cell_rows >= 3)
        & (cell_rows < tile_side + 3)
        & (cell_cols >= 3)
        & (cell_cols < tile_side + 3)
    )
    outside = (~inside).reshape(-1)
    return (cell_rows.reshape(-1)[outside], cell_cols.reshape(-1)[outside])


def depthwise(field_in, kern_in):
    return lax.conv_general_dilated(
        field_in,
        kern_in,
        (1, 1),
        "VALID",
        dimension_numbers=("NHWC", "HWIO", "NHWC"),
        feature_group_count=field_in.shape[-1],
        precision=lax.Precision.HIGHEST,
    )


def assemble(tile, cycle_data):
    side = tile.shape[0]
    wide = side + 6
    channels = tile.shape[-1]
    band = 3 * wide
    top = cycle_data[:band].reshape(3, wide, channels)
    middle = cycle_data[band : band + 6 * side].reshape(side, 6, channels)
    bottom = cycle_data[band + 6 * side :].reshape(3, wide, channels)
    centre = jnp.concatenate([middle[:, :3], tile, middle[:, 3:]], axis=1)
    return jnp.concatenate([top, centre, bottom], axis=0)


def ring_of(square, side):
    channels = square.shape[-1]
    top = square[:3].reshape(-1, channels)
    middle = jnp.concatenate([square[3 : side + 3, :3], square[3 : side + 3, side + 3 :]], axis=1)
    bottom = square[side + 3 :].reshape(-1, channels)
    return jnp.concatenate([top, middle.reshape(-1, channels), bottom], axis=0)


def normal_cdf(values):
    return 0.5 * (1.0 + lax.erf(values * 0.7071067811865476))


def move_links(blocks, heading):
    ups = [k for k, offset in enumerate(LINK_OFFSETS) if offset[0] == -1]
    downs = [k for k, offset in enumerate(LINK_OFFSETS) if offset[0] == 1]
    moved = list(blocks[k] for k in range(len(LINK_OFFSETS)))
    for group, step in ((ups, -heading), (downs, heading)):
        shifted = from_behind(jnp.stack([moved[k] for k in group]), "face", step)
        for place, k in enumerate(group):
            moved[k] = shifted[place]
    lefts = [k for k, offset in enumerate(LINK_OFFSETS) if offset[1] == -1]
    rights = [k for k, offset in enumerate(LINK_OFFSETS) if offset[1] == 1]
    for group, step in ((lefts, -heading), (rights, heading)):
        shifted = from_behind(jnp.stack([moved[k] for k in group]), "tile", step)
        for place, k in enumerate(group):
            moved[k] = shifted[place]
    return jnp.stack(moved)


def local(
    loader,
    row_tile,
    row_pixel,
    neighbours,
    send_pixels,
    halo_from,
    cotangent,
    kernel,
    conv_bias,
    norm_gain,
    norm_bias,
    weight_in,
    bias_in,
    weight_out,
    bias_out,
    layer_scale,
):
    grid_rows = lax.axis_size("face")
    grid_cols = lax.axis_size("tile")
    tile_count = grid_rows * grid_cols
    pixel_count = loader.shape[1]
    channels = loader.shape[2]
    capacity = send_pixels.shape[2]
    per_peer = pixel_count // tile_count
    tile_side = math.isqrt(pixel_count)
    cycle_rows, cycle_cols = cycle_cells(tile_side)
    factor = 1.0 / math.sqrt(lax.axis_size("dp") * tile_count * pixel_count)
    ordering = jnp.argsort(row_tile, stable=True)
    outgoing = loader[0][ordering].reshape(tile_count, per_peer, channels)
    labels = row_pixel[ordering].reshape(tile_count, per_peer)
    digits = jnp.concatenate([labels // 32, labels % 32], axis=1).astype(loader.dtype)
    label_row = jnp.pad(digits, ((0, 0), (0, channels - 2 * per_peer)))[:, None, :]
    parcel = lax.all_to_all(
        jnp.concatenate([outgoing, label_row], axis=1),
        ("face", "tile"),
        split_axis=0,
        concat_axis=0,
        tiled=True,
    )
    arrived = parcel[:, :per_peer]
    got = parcel[:, per_peer, : 2 * per_peer].astype(jnp.int32)
    places = got[:, :per_peer] * 32 + got[:, per_peer:]
    field = (
        jnp.zeros((pixel_count, channels), loader.dtype)
        .at[places.reshape(-1)]
        .set(arrived.reshape(-1, channels))
    )
    my_row = lax.axis_index("face")
    my_col = lax.axis_index("tile")
    row_steps = jnp.asarray([offset[0] for offset in LINK_OFFSETS], jnp.int32)
    col_steps = jnp.asarray([offset[1] for offset in LINK_OFFSETS], jnp.int32)
    sources = (my_row - row_steps) % grid_rows * grid_cols + (my_col - col_steps) % grid_cols
    senders = halo_from[0] // capacity
    matching = senders[:, None] == sources[None, :]
    link_of = jnp.sum(matching.astype(jnp.int32) * jnp.arange(8, dtype=jnp.int32)[None, :], axis=1)
    readable = jnp.any(matching, axis=1)
    recv_index = jnp.where(readable, link_of * capacity + halo_from[0] % capacity, 8 * capacity)
    live = (neighbours[0] < tile_count)[:, None, None]
    extended = jnp.concatenate([field, jnp.zeros((1, channels), field.dtype)], axis=0)
    blocks_out = jnp.where(live, extended[send_pixels[0]], jnp.zeros((), field.dtype))
    received = move_links(blocks_out, 1)
    flat_recv = jnp.concatenate(
        [received.reshape(8 * capacity, channels), jnp.zeros((1, channels), field.dtype)], axis=0
    )
    cycle_data = flat_recv[recv_index]
    padded = assemble(field.reshape(tile_side, tile_side, channels), cycle_data)
    kern_f = kernel.astype(jnp.float32).reshape(7, 7, 1, channels)
    conv_out, conv_back = jax.vjp(depthwise, padded.astype(jnp.float32)[None], kern_f)
    mixed = conv_out.reshape(pixel_count, channels) + conv_bias
    average = jnp.mean(mixed, axis=-1, keepdims=True)
    centred = mixed - average
    inv_scale = lax.rsqrt(jnp.mean(centred * centred, axis=-1, keepdims=True) + 1e-06)
    standard = centred * inv_scale
    normed = (standard * norm_gain + norm_bias).astype(jnp.bfloat16)
    hidden = jnp.dot(normed, weight_in, preferred_element_type=jnp.float32) + bias_in
    cdf_vals = normal_cdf(hidden)
    active = (hidden * cdf_vals).astype(jnp.bfloat16)
    branch = jnp.dot(active, weight_out, preferred_element_type=jnp.float32) + bias_out
    block_out = (field.astype(jnp.float32) + layer_scale * branch).astype(jnp.bfloat16)
    grad_f = cotangent[0].astype(jnp.float32)
    g_scale = jnp.sum(grad_f * branch, axis=0) * factor
    d_branch = (grad_f * layer_scale).astype(jnp.bfloat16)
    g_w_out = jnp.dot(active.T, d_branch, preferred_element_type=jnp.float32) * factor
    g_b_out = jnp.sum(d_branch.astype(jnp.float32), axis=0) * factor
    d_active = jnp.dot(d_branch, weight_out.T, preferred_element_type=jnp.float32)
    slope = cdf_vals + hidden * jnp.exp(-0.5 * hidden * hidden) * 0.3989422804014327
    d_hidden = (d_active * slope).astype(jnp.bfloat16)
    g_w_in = jnp.dot(normed.T, d_hidden, preferred_element_type=jnp.float32) * factor
    g_b_in = jnp.sum(d_hidden.astype(jnp.float32), axis=0) * factor
    d_normed = jnp.dot(d_hidden, weight_in.T, preferred_element_type=jnp.float32)
    g_gain = jnp.sum(d_normed * standard, axis=0) * factor
    g_nbias = jnp.sum(d_normed, axis=0) * factor
    scaled = d_normed * norm_gain
    d_mixed = (
        inv_scale
        * (
            scaled
            - jnp.mean(scaled, axis=-1, keepdims=True)
            - standard * jnp.mean(scaled * standard, axis=-1, keepdims=True)
        )
    ).astype(jnp.bfloat16)
    g_cbias = jnp.sum(d_mixed.astype(jnp.float32), axis=0) * factor
    d_pad, g_kern = conv_back(
        d_mixed.astype(jnp.float32).reshape(1, tile_side, tile_side, channels)
    )
    d_pad = d_pad[0]
    g_kern = g_kern.reshape(49, channels) * factor
    inner_grad = d_pad[3 : tile_side + 3, 3 : tile_side + 3].reshape(pixel_count, channels)
    cycle_grad = ring_of(d_pad, tile_side).astype(jnp.bfloat16)
    back_parcel = (
        jnp.zeros((8 * capacity + 1, channels), jnp.bfloat16).at[recv_index].set(cycle_grad)
    )
    back_parcel = back_parcel[: 8 * capacity].reshape(8, capacity, channels)
    returned = move_links(back_parcel, -1)
    returned = jnp.where(live, returned, jnp.zeros((), returned.dtype))
    incoming = (
        jnp.zeros((pixel_count + 1, channels), jnp.float32)
        .at[send_pixels[0].reshape(-1)]
        .add(returned.reshape(-1, channels).astype(jnp.float32))
    )
    field_grad = (grad_f + inner_grad + incoming[:pixel_count]).astype(jnp.bfloat16)
    g_kern, g_cbias, g_gain, g_nbias, g_w_in, g_b_in, g_w_out, g_b_out, g_scale = tree_sum(
        (g_kern, g_cbias, g_gain, g_nbias, g_w_in, g_b_in, g_w_out, g_b_out, g_scale),
        ("dp", "tile"),
        ("face",),
    )
    return (
        block_out[None],
        field_grad[None],
        g_kern,
        g_cbias,
        g_gain,
        g_nbias,
        g_w_in,
        g_b_in,
        g_w_out,
        g_b_out,
        g_scale,
    )


def solution(mesh):
    placed = (
        P("dp", ("face", "tile"), None),
        P(("face", "tile")),
        P(("face", "tile")),
        P(("face", "tile"), None),
        P(("face", "tile"), None, None),
        P(("face", "tile"), None),
        P("dp", ("face", "tile"), None),
        P(),
        P(),
        P(),
        P(),
        P(),
        P(),
        P(),
        P(),
        P(),
    )
    return jax.shard_map(
        local,
        mesh=mesh,
        in_specs=placed,
        out_specs=(
            P("dp", ("face", "tile"), None),
            P("dp", ("face", "tile"), None),
            P(),
            P(),
            P(),
            P(),
            P(),
            P(),
            P(),
            P(),
            P(),
        ),
        check_vma=False,
    )
```

```python
import math

import jax
import jax.numpy as jnp
import numpy as np
from jax import lax
from jax.sharding import PartitionSpec as P

LINK_OFFSETS = ((-1, -1), (-1, 0), (-1, 1), (0, -1), (0, 1), (1, -1), (1, 0), (1, 1))


def from_behind(value, axis, steps):
    count = lax.axis_size(axis)
    pairs = [(source, (source + steps) % count) for source in range(count)]
    return lax.ppermute(value, axis, pairs)


def tree_sum(parts, halving_axes, doubling_axes):
    flat = jnp.concatenate([part.reshape(-1) for part in parts])

    def bits_of(axes):
        steps = []
        for axis in axes:
            size = lax.axis_size(axis)
            bit = 1
            while bit < size:
                steps.append((axis, bit, size))
                bit *= 2
        return steps

    halving = bits_of(halving_axes)
    total = flat.shape[0]
    pad = (-total) % (1 << len(halving))
    buf = jnp.pad(flat, (0, pad))
    for axis, bit, size in halving:
        upper = (lax.axis_index(axis) // bit) % 2 == 1
        half = buf.shape[0] // 2
        low, high = buf[:half], buf[half:]
        keep = jnp.where(upper, high, low)
        send = jnp.where(upper, low, high)
        pairs = [(i, i ^ bit) for i in range(size)]
        buf = keep + lax.ppermute(send, axis, pairs)
    for axis, bit, size in bits_of(doubling_axes):
        buf = buf + lax.ppermute(buf, axis, [(i, i ^ bit) for i in range(size)])
    for axis, bit, size in reversed(halving):
        upper = (lax.axis_index(axis) // bit) % 2 == 1
        pairs = [(i, i ^ bit) for i in range(size)]
        got = lax.ppermute(buf, axis, pairs)
        buf = jnp.where(upper, jnp.concatenate([got, buf]), jnp.concatenate([buf, got]))
    out = []
    start = 0
    for part in parts:
        out.append(buf[start : start + part.size].reshape(part.shape))
        start += part.size
    return tuple(out)

def cycle_cells(tile_side):
    padded_side = tile_side + 6
    cell_rows, cell_cols = np.meshgrid(
        np.arange(padded_side), np.arange(padded_side), indexing="ij"
    )
    inside = (
        (cell_rows >= 3)
        & (cell_rows < tile_side + 3)
        & (cell_cols >= 3)
        & (cell_cols < tile_side + 3)
    )
    outside = (~inside).reshape(-1)
    return (cell_rows.reshape(-1)[outside], cell_cols.reshape(-1)[outside])


def depthwise(field_in, kern_in):
    return lax.conv_general_dilated(
        field_in,
        kern_in,
        (1, 1),
        "VALID",
        dimension_numbers=("NHWC", "HWIO", "NHWC"),
        feature_group_count=field_in.shape[-1],
        precision=lax.Precision.HIGHEST,
    )


def assemble(tile, cycle_data):
    side = tile.shape[0]
    wide = side + 6
    channels = tile.shape[-1]
    band = 3 * wide
    top = cycle_data[:band].reshape(3, wide, channels)
    middle = cycle_data[band : band + 6 * side].reshape(side, 6, channels)
    bottom = cycle_data[band + 6 * side :].reshape(3, wide, channels)
    centre = jnp.concatenate([middle[:, :3], tile, middle[:, 3:]], axis=1)
    return jnp.concatenate([top, centre, bottom], axis=0)


def ring_of(square, side):
    channels = square.shape[-1]
    top = square[:3].reshape(-1, channels)
    middle = jnp.concatenate([square[3 : side + 3, :3], square[3 : side + 3, side + 3 :]], axis=1)
    bottom = square[side + 3 :].reshape(-1, channels)
    return jnp.concatenate([top, middle.reshape(-1, channels), bottom], axis=0)


def shifted_conv(square, kern, out_side):
    total = None
    for di in range(7):
        for dj in range(7):
            term = square[di : di + out_side, dj : dj + out_side] * kern[di, dj]
            total = term if total is None else total + term
    return total


def tap_sums(square, d_square, side):
    return jnp.stack(
        [
            jnp.sum(square[di : di + side, dj : dj + side] * d_square, axis=(0, 1))
            for di in range(7)
            for dj in range(7)
        ]
    )


def normal_cdf(values):
    return 0.5 * (1.0 + lax.erf(values * 0.7071067811865476))


def move_links(blocks, heading):
    ups = [k for k, offset in enumerate(LINK_OFFSETS) if offset[0] == -1]
    downs = [k for k, offset in enumerate(LINK_OFFSETS) if offset[0] == 1]
    moved = list(blocks[k] for k in range(len(LINK_OFFSETS)))
    for group, step in ((ups, -heading), (downs, heading)):
        shifted = from_behind(jnp.stack([moved[k] for k in group]), "face", step)
        for place, k in enumerate(group):
            moved[k] = shifted[place]
    lefts = [k for k, offset in enumerate(LINK_OFFSETS) if offset[1] == -1]
    rights = [k for k, offset in enumerate(LINK_OFFSETS) if offset[1] == 1]
    for group, step in ((lefts, -heading), (rights, heading)):
        shifted = from_behind(jnp.stack([moved[k] for k in group]), "tile", step)
        for place, k in enumerate(group):
            moved[k] = shifted[place]
    return jnp.stack(moved)


def local(
    loader,
    row_tile,
    row_pixel,
    neighbours,
    send_pixels,
    halo_from,
    cotangent,
    kernel,
    conv_bias,
    norm_gain,
    norm_bias,
    weight_in,
    bias_in,
    weight_out,
    bias_out,
    layer_scale,
):
    grid_rows = lax.axis_size("face")
    grid_cols = lax.axis_size("tile")
    tile_count = grid_rows * grid_cols
    pixel_count = loader.shape[1]
    channels = loader.shape[2]
    capacity = send_pixels.shape[2]
    per_peer = pixel_count // tile_count
    tile_side = math.isqrt(pixel_count)
    cycle_rows, cycle_cols = cycle_cells(tile_side)
    factor = 1.0 / math.sqrt(lax.axis_size("dp") * tile_count * pixel_count)
    ordering = jnp.argsort(row_tile, stable=True)
    outgoing = loader[0][ordering].reshape(tile_count, per_peer, channels)
    labels = row_pixel[ordering].reshape(tile_count, per_peer)
    digits = jnp.concatenate([labels // 32, labels % 32], axis=1).astype(loader.dtype)
    label_row = jnp.pad(digits, ((0, 0), (0, channels - 2 * per_peer)))[:, None, :]
    parcel = lax.all_to_all(
        jnp.concatenate([outgoing, label_row], axis=1),
        ("face", "tile"),
        split_axis=0,
        concat_axis=0,
        tiled=True,
    )
    arrived = parcel[:, :per_peer]
    got = parcel[:, per_peer, : 2 * per_peer].astype(jnp.int32)
    places = got[:, :per_peer] * 32 + got[:, per_peer:]
    field = (
        jnp.zeros((pixel_count, channels), loader.dtype)
        .at[places.reshape(-1)]
        .set(arrived.reshape(-1, channels))
    )
    my_row = lax.axis_index("face")
    my_col = lax.axis_index("tile")
    row_steps = jnp.asarray([offset[0] for offset in LINK_OFFSETS], jnp.int32)
    col_steps = jnp.asarray([offset[1] for offset in LINK_OFFSETS], jnp.int32)
    sources = (my_row - row_steps) % grid_rows * grid_cols + (my_col - col_steps) % grid_cols
    senders = halo_from[0] // capacity
    matching = senders[:, None] == sources[None, :]
    link_of = jnp.sum(matching.astype(jnp.int32) * jnp.arange(8, dtype=jnp.int32)[None, :], axis=1)
    readable = jnp.any(matching, axis=1)
    recv_index = jnp.where(readable, link_of * capacity + halo_from[0] % capacity, 8 * capacity)
    live = (neighbours[0] < tile_count)[:, None, None]
    extended = jnp.concatenate([field, jnp.zeros((1, channels), field.dtype)], axis=0)
    blocks_out = jnp.where(live, extended[send_pixels[0]], jnp.zeros((), field.dtype))
    received = move_links(blocks_out, 1)
    flat_recv = jnp.concatenate(
        [received.reshape(8 * capacity, channels), jnp.zeros((1, channels), field.dtype)], axis=0
    )
    cycle_data = flat_recv[recv_index]
    padded = assemble(field.reshape(tile_side, tile_side, channels), cycle_data)
    kern_f = kernel.astype(jnp.float32).reshape(7, 7, channels)
    padded_f = padded.astype(jnp.float32)
    mixed = shifted_conv(padded_f, kern_f, tile_side).reshape(pixel_count, channels) + conv_bias
    average = jnp.mean(mixed, axis=-1, keepdims=True)
    centred = mixed - average
    inv_scale = lax.rsqrt(jnp.mean(centred * centred, axis=-1, keepdims=True) + 1e-06)
    standard = centred * inv_scale
    normed = (standard * norm_gain + norm_bias).astype(jnp.bfloat16)
    hidden = jnp.dot(normed, weight_in, preferred_element_type=jnp.float32) + bias_in
    cdf_vals = normal_cdf(hidden)
    active = (hidden * cdf_vals).astype(jnp.bfloat16)
    branch = jnp.dot(active, weight_out, preferred_element_type=jnp.float32) + bias_out
    block_out = (field.astype(jnp.float32) + layer_scale * branch).astype(jnp.bfloat16)
    grad_f = cotangent[0].astype(jnp.float32)
    g_scale = jnp.sum(grad_f * branch, axis=0) * factor
    d_branch = (grad_f * layer_scale).astype(jnp.bfloat16)
    g_w_out = jnp.dot(active.T, d_branch, preferred_element_type=jnp.float32) * factor
    g_b_out = jnp.sum(d_branch.astype(jnp.float32), axis=0) * factor
    d_active = jnp.dot(d_branch, weight_out.T, preferred_element_type=jnp.float32)
    slope = cdf_vals + hidden * jnp.exp(-0.5 * hidden * hidden) * 0.3989422804014327
    d_hidden = (d_active * slope).astype(jnp.bfloat16)
    g_w_in = jnp.dot(normed.T, d_hidden, preferred_element_type=jnp.float32) * factor
    g_b_in = jnp.sum(d_hidden.astype(jnp.float32), axis=0) * factor
    d_normed = jnp.dot(d_hidden, weight_in.T, preferred_element_type=jnp.float32)
    g_gain = jnp.sum(d_normed * standard, axis=0) * factor
    g_nbias = jnp.sum(d_normed, axis=0) * factor
    scaled = d_normed * norm_gain
    d_mixed = (
        inv_scale
        * (
            scaled
            - jnp.mean(scaled, axis=-1, keepdims=True)
            - standard * jnp.mean(scaled * standard, axis=-1, keepdims=True)
        )
    ).astype(jnp.bfloat16)
    g_cbias = jnp.sum(d_mixed.astype(jnp.float32), axis=0) * factor
    d_square = d_mixed.astype(jnp.float32).reshape(tile_side, tile_side, channels)
    d_pad = shifted_conv(
        jnp.pad(d_square, ((6, 6), (6, 6), (0, 0))), kern_f[::-1, ::-1], tile_side + 6
    )
    g_kern = tap_sums(padded_f, d_square, tile_side) * factor
    inner_grad = d_pad[3 : tile_side + 3, 3 : tile_side + 3].reshape(pixel_count, channels)
    cycle_grad = ring_of(d_pad, tile_side).astype(jnp.bfloat16)
    back_parcel = (
        jnp.zeros((8 * capacity + 1, channels), jnp.bfloat16).at[recv_index].set(cycle_grad)
    )
    back_parcel = back_parcel[: 8 * capacity].reshape(8, capacity, channels)
    returned = move_links(back_parcel, -1)
    returned = jnp.where(live, returned, jnp.zeros((), returned.dtype))
    incoming = (
        jnp.zeros((pixel_count + 1, channels), jnp.float32)
        .at[send_pixels[0].reshape(-1)]
        .add(returned.reshape(-1, channels).astype(jnp.float32))
    )
    field_grad = (grad_f + inner_grad + incoming[:pixel_count]).astype(jnp.bfloat16)
    g_kern, g_cbias, g_gain, g_nbias, g_w_in, g_b_in, g_w_out, g_b_out, g_scale = tree_sum(
        (g_kern, g_cbias, g_gain, g_nbias, g_w_in, g_b_in, g_w_out, g_b_out, g_scale),
        ("dp", "tile"),
        ("face",),
    )
    return (
        block_out[None],
        field_grad[None],
        g_kern,
        g_cbias,
        g_gain,
        g_nbias,
        g_w_in,
        g_b_in,
        g_w_out,
        g_b_out,
        g_scale,
    )


def solution(mesh):
    placed = (
        P("dp", ("face", "tile"), None),
        P(("face", "tile")),
        P(("face", "tile")),
        P(("face", "tile"), None),
        P(("face", "tile"), None, None),
        P(("face", "tile"), None),
        P("dp", ("face", "tile"), None),
        P(),
        P(),
        P(),
        P(),
        P(),
        P(),
        P(),
        P(),
        P(),
    )
    return jax.shard_map(
        local,
        mesh=mesh,
        in_specs=placed,
        out_specs=(
            P("dp", ("face", "tile"), None),
            P("dp", ("face", "tile"), None),
            P(),
            P(),
            P(),
            P(),
            P(),
            P(),
            P(),
            P(),
            P(),
        ),
        check_vma=False,
    )
```

```python
import math

import jax
import jax.numpy as jnp
import numpy as np
from jax import lax
from jax.sharding import PartitionSpec as P

LINK_OFFSETS = ((-1, -1), (-1, 0), (-1, 1), (0, -1), (0, 1), (1, -1), (1, 0), (1, 1))


def from_behind(value, axis, steps):
    count = lax.axis_size(axis)
    pairs = [(source, (source + steps) % count) for source in range(count)]
    return lax.ppermute(value, axis, pairs)


def tree_sum(parts, halving_axes, doubling_axes, rider=None, stages=()):
    flat = jnp.concatenate([part.reshape(-1) for part in parts])

    def bits_of(axes):
        steps = []
        for axis in axes:
            size = lax.axis_size(axis)
            bit = 1
            while bit < size:
                steps.append((axis, bit, size))
                bit *= 2
        return steps

    halving = bits_of(halving_axes)
    plan = dict(stages)
    count = [0]

    def stepped(buf):
        nonlocal rider
        count[0] += 1
        if count[0] in plan:
            buf, rider = lax.optimization_barrier((buf, rider))
            rider = plan[count[0]](rider)
        return buf

    total = flat.shape[0]
    pad = (-total) % (1 << len(halving))
    buf = jnp.pad(flat, (0, pad))
    for axis, bit, size in halving:
        upper = (lax.axis_index(axis) // bit) % 2 == 1
        half = buf.shape[0] // 2
        low, high = buf[:half], buf[half:]
        keep = jnp.where(upper, high, low)
        send = jnp.where(upper, low, high)
        pairs = [(i, i ^ bit) for i in range(size)]
        buf = stepped(keep + lax.ppermute(send, axis, pairs))
    for axis, bit, size in bits_of(doubling_axes):
        buf = stepped(buf + lax.ppermute(buf, axis, [(i, i ^ bit) for i in range(size)]))
    for axis, bit, size in reversed(halving):
        upper = (lax.axis_index(axis) // bit) % 2 == 1
        pairs = [(i, i ^ bit) for i in range(size)]
        got = lax.ppermute(buf, axis, pairs)
        buf = stepped(jnp.where(upper, jnp.concatenate([got, buf]), jnp.concatenate([buf, got])))
    out = []
    start = 0
    for part in parts:
        out.append(buf[start : start + part.size].reshape(part.shape))
        start += part.size
    return tuple(out), rider

def cycle_cells(tile_side):
    padded_side = tile_side + 6
    cell_rows, cell_cols = np.meshgrid(
        np.arange(padded_side), np.arange(padded_side), indexing="ij"
    )
    inside = (
        (cell_rows >= 3)
        & (cell_rows < tile_side + 3)
        & (cell_cols >= 3)
        & (cell_cols < tile_side + 3)
    )
    outside = (~inside).reshape(-1)
    return (cell_rows.reshape(-1)[outside], cell_cols.reshape(-1)[outside])


def depthwise(field_in, kern_in):
    return lax.conv_general_dilated(
        field_in,
        kern_in,
        (1, 1),
        "VALID",
        dimension_numbers=("NHWC", "HWIO", "NHWC"),
        feature_group_count=field_in.shape[-1],
        precision=lax.Precision.HIGHEST,
    )


def assemble(tile, cycle_data):
    side = tile.shape[0]
    wide = side + 6
    channels = tile.shape[-1]
    band = 3 * wide
    top = cycle_data[:band].reshape(3, wide, channels)
    middle = cycle_data[band : band + 6 * side].reshape(side, 6, channels)
    bottom = cycle_data[band + 6 * side :].reshape(3, wide, channels)
    centre = jnp.concatenate([middle[:, :3], tile, middle[:, 3:]], axis=1)
    return jnp.concatenate([top, centre, bottom], axis=0)


def ring_of(square, side):
    channels = square.shape[-1]
    top = square[:3].reshape(-1, channels)
    middle = jnp.concatenate([square[3 : side + 3, :3], square[3 : side + 3, side + 3 :]], axis=1)
    bottom = square[side + 3 :].reshape(-1, channels)
    return jnp.concatenate([top, middle.reshape(-1, channels), bottom], axis=0)


def shifted_conv(square, kern, out_side):
    total = None
    for di in range(7):
        for dj in range(7):
            term = square[di : di + out_side, dj : dj + out_side] * kern[di, dj]
            total = term if total is None else total + term
    return total


def tap_sums(square, d_square, side):
    return jnp.stack(
        [
            jnp.sum(square[di : di + side, dj : dj + side] * d_square, axis=(0, 1))
            for di in range(7)
            for dj in range(7)
        ]
    )


def normal_cdf(values):
    return 0.5 * (1.0 + lax.erf(values * 0.7071067811865476))


def move_round(blocks, heading, axis):
    along = 0 if axis == "face" else 1
    moved = list(blocks[k] for k in range(len(LINK_OFFSETS)))
    for sign in (-1, 1):
        group = [k for k, offset in enumerate(LINK_OFFSETS) if offset[along] == sign]
        shifted = from_behind(jnp.stack([moved[k] for k in group]), axis, sign * heading)
        for place, k in enumerate(group):
            moved[k] = shifted[place]
    return jnp.stack(moved)


def move_links(blocks, heading):
    return move_round(move_round(blocks, heading, "face"), heading, "tile")


def local(
    loader,
    row_tile,
    row_pixel,
    neighbours,
    send_pixels,
    halo_from,
    cotangent,
    kernel,
    conv_bias,
    norm_gain,
    norm_bias,
    weight_in,
    bias_in,
    weight_out,
    bias_out,
    layer_scale,
):
    grid_rows = lax.axis_size("face")
    grid_cols = lax.axis_size("tile")
    tile_count = grid_rows * grid_cols
    pixel_count = loader.shape[1]
    channels = loader.shape[2]
    capacity = send_pixels.shape[2]
    per_peer = pixel_count // tile_count
    tile_side = math.isqrt(pixel_count)
    cycle_rows, cycle_cols = cycle_cells(tile_side)
    factor = 1.0 / math.sqrt(lax.axis_size("dp") * tile_count * pixel_count)
    ordering = jnp.argsort(row_tile, stable=True)
    outgoing = loader[0][ordering].reshape(tile_count, per_peer, channels)
    labels = row_pixel[ordering].reshape(tile_count, per_peer)
    digits = jnp.concatenate([labels // 32, labels % 32], axis=1).astype(loader.dtype)
    label_row = jnp.pad(digits, ((0, 0), (0, channels - 2 * per_peer)))[:, None, :]
    parcel = lax.all_to_all(
        jnp.concatenate([outgoing, label_row], axis=1),
        ("face", "tile"),
        split_axis=0,
        concat_axis=0,
        tiled=True,
    )
    arrived = parcel[:, :per_peer]
    got = parcel[:, per_peer, : 2 * per_peer].astype(jnp.int32)
    places = got[:, :per_peer] * 32 + got[:, per_peer:]
    field = (
        jnp.zeros((pixel_count, channels), loader.dtype)
        .at[places.reshape(-1)]
        .set(arrived.reshape(-1, channels))
    )
    my_row = lax.axis_index("face")
    my_col = lax.axis_index("tile")
    row_steps = jnp.asarray([offset[0] for offset in LINK_OFFSETS], jnp.int32)
    col_steps = jnp.asarray([offset[1] for offset in LINK_OFFSETS], jnp.int32)
    sources = (my_row - row_steps) % grid_rows * grid_cols + (my_col - col_steps) % grid_cols
    senders = halo_from[0] // capacity
    matching = senders[:, None] == sources[None, :]
    link_of = jnp.sum(matching.astype(jnp.int32) * jnp.arange(8, dtype=jnp.int32)[None, :], axis=1)
    readable = jnp.any(matching, axis=1)
    recv_index = jnp.where(readable, link_of * capacity + halo_from[0] % capacity, 8 * capacity)
    live = (neighbours[0] < tile_count)[:, None, None]
    extended = jnp.concatenate([field, jnp.zeros((1, channels), field.dtype)], axis=0)
    blocks_out = jnp.where(live, extended[send_pixels[0]], jnp.zeros((), field.dtype))
    received = move_links(blocks_out, 1)
    flat_recv = jnp.concatenate(
        [received.reshape(8 * capacity, channels), jnp.zeros((1, channels), field.dtype)], axis=0
    )
    cycle_data = flat_recv[recv_index]
    padded = assemble(field.reshape(tile_side, tile_side, channels), cycle_data)
    kern_f = kernel.astype(jnp.float32).reshape(7, 7, channels)
    padded_f = padded.astype(jnp.float32)
    mixed = shifted_conv(padded_f, kern_f, tile_side).reshape(pixel_count, channels) + conv_bias
    average = jnp.mean(mixed, axis=-1, keepdims=True)
    centred = mixed - average
    inv_scale = lax.rsqrt(jnp.mean(centred * centred, axis=-1, keepdims=True) + 1e-06)
    standard = centred * inv_scale
    normed = (standard * norm_gain + norm_bias).astype(jnp.bfloat16)
    hidden = jnp.dot(normed, weight_in, preferred_element_type=jnp.float32) + bias_in
    cdf_vals = normal_cdf(hidden)
    active = (hidden * cdf_vals).astype(jnp.bfloat16)
    branch = jnp.dot(active, weight_out, preferred_element_type=jnp.float32) + bias_out
    block_out = (field.astype(jnp.float32) + layer_scale * branch).astype(jnp.bfloat16)
    grad_f = cotangent[0].astype(jnp.float32)
    g_scale = jnp.sum(grad_f * branch, axis=0) * factor
    d_branch = (grad_f * layer_scale).astype(jnp.bfloat16)
    g_w_out = jnp.dot(active.T, d_branch, preferred_element_type=jnp.float32) * factor
    g_b_out = jnp.sum(d_branch.astype(jnp.float32), axis=0) * factor
    d_active = jnp.dot(d_branch, weight_out.T, preferred_element_type=jnp.float32)
    slope = cdf_vals + hidden * jnp.exp(-0.5 * hidden * hidden) * 0.3989422804014327
    d_hidden = (d_active * slope).astype(jnp.bfloat16)
    g_w_in = jnp.dot(normed.T, d_hidden, preferred_element_type=jnp.float32) * factor
    g_b_in = jnp.sum(d_hidden.astype(jnp.float32), axis=0) * factor
    d_normed = jnp.dot(d_hidden, weight_in.T, preferred_element_type=jnp.float32)
    g_gain = jnp.sum(d_normed * standard, axis=0) * factor
    g_nbias = jnp.sum(d_normed, axis=0) * factor
    scaled = d_normed * norm_gain
    d_mixed = (
        inv_scale
        * (
            scaled
            - jnp.mean(scaled, axis=-1, keepdims=True)
            - standard * jnp.mean(scaled * standard, axis=-1, keepdims=True)
        )
    ).astype(jnp.bfloat16)
    g_cbias = jnp.sum(d_mixed.astype(jnp.float32), axis=0) * factor
    d_square = d_mixed.astype(jnp.float32).reshape(tile_side, tile_side, channels)
    d_pad = shifted_conv(
        jnp.pad(d_square, ((6, 6), (6, 6), (0, 0))), kern_f[::-1, ::-1], tile_side + 6
    )
    g_kern = tap_sums(padded_f, d_square, tile_side) * factor
    inner_grad = d_pad[3 : tile_side + 3, 3 : tile_side + 3].reshape(pixel_count, channels)
    cycle_grad = ring_of(d_pad, tile_side).astype(jnp.bfloat16)
    back_parcel = (
        jnp.zeros((8 * capacity + 1, channels), jnp.bfloat16).at[recv_index].set(cycle_grad)
    )
    back_parcel = back_parcel[: 8 * capacity].reshape(8, capacity, channels)

    def finish(moved):
        returned = jnp.where(live, moved, jnp.zeros((), moved.dtype))
        incoming = (
            jnp.zeros((pixel_count + 1, channels), jnp.float32)
            .at[send_pixels[0].reshape(-1)]
            .add(returned.reshape(-1, channels).astype(jnp.float32))
        )
        return (grad_f + inner_grad + incoming[:pixel_count]).astype(jnp.bfloat16)

    sums, field_grad = tree_sum(
        (g_kern, g_cbias, g_gain, g_nbias, g_w_in, g_b_in, g_w_out, g_b_out, g_scale),
        ("dp", "tile"),
        ("face",),
        rider=back_parcel,
        stages=(
            (1, lambda parcel: move_round(parcel, -1, "face")),
            (3, lambda parcel: move_round(parcel, -1, "tile")),
            (5, finish),
        ),
    )
    g_kern, g_cbias, g_gain, g_nbias, g_w_in, g_b_in, g_w_out, g_b_out, g_scale = sums
    return (
        block_out[None],
        field_grad[None],
        g_kern,
        g_cbias,
        g_gain,
        g_nbias,
        g_w_in,
        g_b_in,
        g_w_out,
        g_b_out,
        g_scale,
    )


def solution(mesh):
    placed = (
        P("dp", ("face", "tile"), None),
        P(("face", "tile")),
        P(("face", "tile")),
        P(("face", "tile"), None),
        P(("face", "tile"), None, None),
        P(("face", "tile"), None),
        P("dp", ("face", "tile"), None),
        P(),
        P(),
        P(),
        P(),
        P(),
        P(),
        P(),
        P(),
        P(),
    )
    return jax.shard_map(
        local,
        mesh=mesh,
        in_specs=placed,
        out_specs=(
            P("dp", ("face", "tile"), None),
            P("dp", ("face", "tile"), None),
            P(),
            P(),
            P(),
            P(),
            P(),
            P(),
            P(),
            P(),
            P(),
        ),
        check_vma=False,
    )
```

```python
import math

import jax
import jax.numpy as jnp
import numpy as np
from jax import lax
from jax.sharding import PartitionSpec as P

LINK_OFFSETS = ((-1, -1), (-1, 0), (-1, 1), (0, -1), (0, 1), (1, -1), (1, 0), (1, 1))


def from_behind(value, axis, steps):
    count = lax.axis_size(axis)
    pairs = [(source, (source + steps) % count) for source in range(count)]
    return lax.ppermute(value, axis, pairs)


def tree_sum(parts, halving_axes, doubling_axes, rider=None, stages=()):
    flat = jnp.concatenate([part.reshape(-1) for part in parts])

    def bits_of(axes):
        steps = []
        for axis in axes:
            size = lax.axis_size(axis)
            bit = 1
            while bit < size:
                steps.append((axis, bit, size))
                bit *= 2
        return steps

    halving = bits_of(halving_axes)
    plan = dict(stages)
    count = [0]

    def stepped(buf):
        nonlocal rider
        count[0] += 1
        if count[0] in plan:
            buf, rider = lax.optimization_barrier((buf, rider))
            rider = plan[count[0]](rider)
        return buf

    total = flat.shape[0]
    pad = (-total) % (1 << len(halving))
    buf = jnp.pad(flat, (0, pad))
    for axis in halving_axes:
        size = lax.axis_size(axis)
        digit = lax.axis_index(axis)
        chunks = jnp.split(buf, size)

        def chunk_at(index):
            chosen = chunks[size - 1]
            for place in reversed(range(size - 1)):
                chosen = jnp.where(index == place, chunks[place], chosen)
            return chosen

        total_chunk = chunk_at(digit)
        for flip in range(1, size):
            pairs = [(i, i ^ flip) for i in range(size)]
            total_chunk = total_chunk + lax.ppermute(chunk_at(digit ^ flip), axis, pairs)
        buf = stepped(total_chunk)
    for axis, bit, size in bits_of(doubling_axes):
        buf = stepped(buf + lax.ppermute(buf, axis, [(i, i ^ bit) for i in range(size)]))
    for axis in reversed(halving_axes):
        size = lax.axis_size(axis)
        digit = lax.axis_index(axis)
        pieces = [buf] + [
            lax.ppermute(buf, axis, [(i, i ^ flip) for i in range(size)]) for flip in range(1, size)
        ]
        placed = []
        for place in range(size):
            source = place ^ digit
            chosen = pieces[size - 1]
            for flip in reversed(range(size - 1)):
                chosen = jnp.where(source == flip, pieces[flip], chosen)
            placed.append(chosen)
        buf = stepped(jnp.concatenate(placed))
    out = []
    start = 0
    for part in parts:
        out.append(buf[start : start + part.size].reshape(part.shape))
        start += part.size
    return tuple(out), rider

def cycle_cells(tile_side):
    padded_side = tile_side + 6
    cell_rows, cell_cols = np.meshgrid(
        np.arange(padded_side), np.arange(padded_side), indexing="ij"
    )
    inside = (
        (cell_rows >= 3)
        & (cell_rows < tile_side + 3)
        & (cell_cols >= 3)
        & (cell_cols < tile_side + 3)
    )
    outside = (~inside).reshape(-1)
    return (cell_rows.reshape(-1)[outside], cell_cols.reshape(-1)[outside])


def depthwise(field_in, kern_in):
    return lax.conv_general_dilated(
        field_in,
        kern_in,
        (1, 1),
        "VALID",
        dimension_numbers=("NHWC", "HWIO", "NHWC"),
        feature_group_count=field_in.shape[-1],
        precision=lax.Precision.HIGHEST,
    )


def assemble(tile, cycle_data):
    side = tile.shape[0]
    wide = side + 6
    channels = tile.shape[-1]
    band = 3 * wide
    top = cycle_data[:band].reshape(3, wide, channels)
    middle = cycle_data[band : band + 6 * side].reshape(side, 6, channels)
    bottom = cycle_data[band + 6 * side :].reshape(3, wide, channels)
    centre = jnp.concatenate([middle[:, :3], tile, middle[:, 3:]], axis=1)
    return jnp.concatenate([top, centre, bottom], axis=0)


def ring_of(square, side):
    channels = square.shape[-1]
    top = square[:3].reshape(-1, channels)
    middle = jnp.concatenate([square[3 : side + 3, :3], square[3 : side + 3, side + 3 :]], axis=1)
    bottom = square[side + 3 :].reshape(-1, channels)
    return jnp.concatenate([top, middle.reshape(-1, channels), bottom], axis=0)


def shifted_conv(square, kern, out_side):
    total = None
    for di in range(7):
        for dj in range(7):
            term = square[di : di + out_side, dj : dj + out_side] * kern[di, dj]
            total = term if total is None else total + term
    return total


def tap_sums(square, d_square, side):
    return jnp.stack(
        [
            jnp.sum(square[di : di + side, dj : dj + side] * d_square, axis=(0, 1))
            for di in range(7)
            for dj in range(7)
        ]
    )


def normal_cdf(values):
    return 0.5 * (1.0 + lax.erf(values * 0.7071067811865476))


def move_round(blocks, heading, axis):
    along = 0 if axis == "face" else 1
    moved = list(blocks[k] for k in range(len(LINK_OFFSETS)))
    for sign in (-1, 1):
        group = [k for k, offset in enumerate(LINK_OFFSETS) if offset[along] == sign]
        shifted = from_behind(jnp.stack([moved[k] for k in group]), axis, sign * heading)
        for place, k in enumerate(group):
            moved[k] = shifted[place]
    return jnp.stack(moved)


def move_links(blocks, heading):
    return move_round(move_round(blocks, heading, "face"), heading, "tile")


def local(
    loader,
    row_tile,
    row_pixel,
    neighbours,
    send_pixels,
    halo_from,
    cotangent,
    kernel,
    conv_bias,
    norm_gain,
    norm_bias,
    weight_in,
    bias_in,
    weight_out,
    bias_out,
    layer_scale,
):
    grid_rows = lax.axis_size("face")
    grid_cols = lax.axis_size("tile")
    tile_count = grid_rows * grid_cols
    pixel_count = loader.shape[1]
    channels = loader.shape[2]
    capacity = send_pixels.shape[2]
    per_peer = pixel_count // tile_count
    tile_side = math.isqrt(pixel_count)
    cycle_rows, cycle_cols = cycle_cells(tile_side)
    factor = 1.0 / math.sqrt(lax.axis_size("dp") * tile_count * pixel_count)
    ordering = jnp.argsort(row_tile, stable=True)
    outgoing = loader[0][ordering].reshape(tile_count, per_peer, channels)
    labels = row_pixel[ordering].reshape(tile_count, per_peer)
    digits = jnp.concatenate([labels // 32, labels % 32], axis=1).astype(loader.dtype)
    label_row = jnp.pad(digits, ((0, 0), (0, channels - 2 * per_peer)))[:, None, :]
    parcel = lax.all_to_all(
        jnp.concatenate([outgoing, label_row], axis=1),
        ("face", "tile"),
        split_axis=0,
        concat_axis=0,
        tiled=True,
    )
    arrived = parcel[:, :per_peer]
    got = parcel[:, per_peer, : 2 * per_peer].astype(jnp.int32)
    places = got[:, :per_peer] * 32 + got[:, per_peer:]
    field = (
        jnp.zeros((pixel_count, channels), loader.dtype)
        .at[places.reshape(-1)]
        .set(arrived.reshape(-1, channels))
    )
    my_row = lax.axis_index("face")
    my_col = lax.axis_index("tile")
    row_steps = jnp.asarray([offset[0] for offset in LINK_OFFSETS], jnp.int32)
    col_steps = jnp.asarray([offset[1] for offset in LINK_OFFSETS], jnp.int32)
    sources = (my_row - row_steps) % grid_rows * grid_cols + (my_col - col_steps) % grid_cols
    senders = halo_from[0] // capacity
    matching = senders[:, None] == sources[None, :]
    link_of = jnp.sum(matching.astype(jnp.int32) * jnp.arange(8, dtype=jnp.int32)[None, :], axis=1)
    readable = jnp.any(matching, axis=1)
    recv_index = jnp.where(readable, link_of * capacity + halo_from[0] % capacity, 8 * capacity)
    live = (neighbours[0] < tile_count)[:, None, None]
    extended = jnp.concatenate([field, jnp.zeros((1, channels), field.dtype)], axis=0)
    blocks_out = jnp.where(live, extended[send_pixels[0]], jnp.zeros((), field.dtype))
    received = move_links(blocks_out, 1)
    flat_recv = jnp.concatenate(
        [received.reshape(8 * capacity, channels), jnp.zeros((1, channels), field.dtype)], axis=0
    )
    cycle_data = flat_recv[recv_index]
    padded = assemble(field.reshape(tile_side, tile_side, channels), cycle_data)
    kern_f = kernel.astype(jnp.float32).reshape(7, 7, channels)
    padded_f = padded.astype(jnp.float32)
    mixed = shifted_conv(padded_f, kern_f, tile_side).reshape(pixel_count, channels) + conv_bias
    average = jnp.mean(mixed, axis=-1, keepdims=True)
    centred = mixed - average
    inv_scale = lax.rsqrt(jnp.mean(centred * centred, axis=-1, keepdims=True) + 1e-06)
    standard = centred * inv_scale
    normed = (standard * norm_gain + norm_bias).astype(jnp.bfloat16)
    hidden = jnp.dot(normed, weight_in, preferred_element_type=jnp.float32) + bias_in
    cdf_vals = normal_cdf(hidden)
    active = (hidden * cdf_vals).astype(jnp.bfloat16)
    branch = jnp.dot(active, weight_out, preferred_element_type=jnp.float32) + bias_out
    block_out = (field.astype(jnp.float32) + layer_scale * branch).astype(jnp.bfloat16)
    grad_f = cotangent[0].astype(jnp.float32)
    g_scale = jnp.sum(grad_f * branch, axis=0) * factor
    d_branch = (grad_f * layer_scale).astype(jnp.bfloat16)
    g_w_out = jnp.dot(active.T, d_branch, preferred_element_type=jnp.float32) * factor
    g_b_out = jnp.sum(d_branch.astype(jnp.float32), axis=0) * factor
    d_active = jnp.dot(d_branch, weight_out.T, preferred_element_type=jnp.float32)
    slope = cdf_vals + hidden * jnp.exp(-0.5 * hidden * hidden) * 0.3989422804014327
    d_hidden = (d_active * slope).astype(jnp.bfloat16)
    g_w_in = jnp.dot(normed.T, d_hidden, preferred_element_type=jnp.float32) * factor
    g_b_in = jnp.sum(d_hidden.astype(jnp.float32), axis=0) * factor
    d_normed = jnp.dot(d_hidden, weight_in.T, preferred_element_type=jnp.float32)
    g_gain = jnp.sum(d_normed * standard, axis=0) * factor
    g_nbias = jnp.sum(d_normed, axis=0) * factor
    scaled = d_normed * norm_gain
    d_mixed = (
        inv_scale
        * (
            scaled
            - jnp.mean(scaled, axis=-1, keepdims=True)
            - standard * jnp.mean(scaled * standard, axis=-1, keepdims=True)
        )
    ).astype(jnp.bfloat16)
    g_cbias = jnp.sum(d_mixed.astype(jnp.float32), axis=0) * factor
    d_square = d_mixed.astype(jnp.float32).reshape(tile_side, tile_side, channels)
    d_pad = shifted_conv(
        jnp.pad(d_square, ((6, 6), (6, 6), (0, 0))), kern_f[::-1, ::-1], tile_side + 6
    )
    g_kern = tap_sums(padded_f, d_square, tile_side) * factor
    inner_grad = d_pad[3 : tile_side + 3, 3 : tile_side + 3].reshape(pixel_count, channels)
    cycle_grad = ring_of(d_pad, tile_side).astype(jnp.bfloat16)
    back_parcel = (
        jnp.zeros((8 * capacity + 1, channels), jnp.bfloat16).at[recv_index].set(cycle_grad)
    )
    back_parcel = back_parcel[: 8 * capacity].reshape(8, capacity, channels)

    def finish(moved):
        returned = jnp.where(live, moved, jnp.zeros((), moved.dtype))
        incoming = (
            jnp.zeros((pixel_count + 1, channels), jnp.float32)
            .at[send_pixels[0].reshape(-1)]
            .add(returned.reshape(-1, channels).astype(jnp.float32))
        )
        return (grad_f + inner_grad + incoming[:pixel_count]).astype(jnp.bfloat16)

    sums, field_grad = tree_sum(
        (g_kern, g_cbias, g_gain, g_nbias, g_w_in, g_b_in, g_w_out, g_b_out, g_scale),
        ("dp", "tile"),
        ("face",),
        rider=back_parcel,
        stages=(
            (1, lambda parcel: move_round(parcel, -1, "face")),
            (3, lambda parcel: move_round(parcel, -1, "tile")),
            (5, finish),
        ),
    )
    g_kern, g_cbias, g_gain, g_nbias, g_w_in, g_b_in, g_w_out, g_b_out, g_scale = sums
    return (
        block_out[None],
        field_grad[None],
        g_kern,
        g_cbias,
        g_gain,
        g_nbias,
        g_w_in,
        g_b_in,
        g_w_out,
        g_b_out,
        g_scale,
    )


def solution(mesh):
    placed = (
        P("dp", ("face", "tile"), None),
        P(("face", "tile")),
        P(("face", "tile")),
        P(("face", "tile"), None),
        P(("face", "tile"), None, None),
        P(("face", "tile"), None),
        P("dp", ("face", "tile"), None),
        P(),
        P(),
        P(),
        P(),
        P(),
        P(),
        P(),
        P(),
        P(),
    )
    return jax.shard_map(
        local,
        mesh=mesh,
        in_specs=placed,
        out_specs=(
            P("dp", ("face", "tile"), None),
            P("dp", ("face", "tile"), None),
            P(),
            P(),
            P(),
            P(),
            P(),
            P(),
            P(),
            P(),
            P(),
        ),
        check_vma=False,
    )
```

```python
import math

import jax
import jax.numpy as jnp
import numpy as np
from jax import lax
from jax.sharding import PartitionSpec as P

LINK_OFFSETS = ((-1, -1), (-1, 0), (-1, 1), (0, -1), (0, 1), (1, -1), (1, 0), (1, 1))


def from_behind(value, axis, steps):
    count = lax.axis_size(axis)
    pairs = [(source, (source + steps) % count) for source in range(count)]
    return lax.ppermute(value, axis, pairs)


def tree_sum(parts, halving_axes, doubling_axes, rider=None, stages=()):
    flat = jnp.concatenate([part.reshape(-1) for part in parts])

    def bits_of(axes):
        steps = []
        for axis in axes:
            size = lax.axis_size(axis)
            bit = 1
            while bit < size:
                steps.append((axis, bit, size))
                bit *= 2
        return steps

    halving = bits_of(halving_axes)
    plan = dict(stages)
    count = [0]

    def stepped(buf):
        nonlocal rider
        count[0] += 1
        if count[0] in plan:
            buf, rider = lax.optimization_barrier((buf, rider))
            rider = plan[count[0]](rider)
        return buf

    total = flat.shape[0]
    pad = (-total) % (1 << len(halving))
    buf = jnp.pad(flat, (0, pad))
    for axis in halving_axes:
        size = lax.axis_size(axis)
        digit = lax.axis_index(axis)
        chunks = jnp.split(buf, size)

        def chunk_at(index):
            chosen = chunks[size - 1]
            for place in reversed(range(size - 1)):
                chosen = jnp.where(index == place, chunks[place], chosen)
            return chosen

        total_chunk = chunk_at(digit)
        for flip in range(1, size):
            pairs = [(i, i ^ flip) for i in range(size)]
            total_chunk = total_chunk + lax.ppermute(chunk_at(digit ^ flip), axis, pairs)
        buf = stepped(total_chunk)
    for axis, bit, size in bits_of(doubling_axes):
        buf = stepped(buf + lax.ppermute(buf, axis, [(i, i ^ bit) for i in range(size)]))
    for axis in reversed(halving_axes):
        size = lax.axis_size(axis)
        digit = lax.axis_index(axis)
        pieces = [buf] + [
            lax.ppermute(buf, axis, [(i, i ^ flip) for i in range(size)]) for flip in range(1, size)
        ]
        placed = []
        for place in range(size):
            source = place ^ digit
            chosen = pieces[size - 1]
            for flip in reversed(range(size - 1)):
                chosen = jnp.where(source == flip, pieces[flip], chosen)
            placed.append(chosen)
        buf = stepped(jnp.concatenate(placed))
    out = []
    start = 0
    for part in parts:
        out.append(buf[start : start + part.size].reshape(part.shape))
        start += part.size
    return tuple(out), rider

def cycle_cells(tile_side):
    padded_side = tile_side + 6
    cell_rows, cell_cols = np.meshgrid(
        np.arange(padded_side), np.arange(padded_side), indexing="ij"
    )
    inside = (
        (cell_rows >= 3)
        & (cell_rows < tile_side + 3)
        & (cell_cols >= 3)
        & (cell_cols < tile_side + 3)
    )
    outside = (~inside).reshape(-1)
    return (cell_rows.reshape(-1)[outside], cell_cols.reshape(-1)[outside])


def depthwise(field_in, kern_in):
    return lax.conv_general_dilated(
        field_in,
        kern_in,
        (1, 1),
        "VALID",
        dimension_numbers=("NHWC", "HWIO", "NHWC"),
        feature_group_count=field_in.shape[-1],
        precision=lax.Precision.HIGHEST,
    )


def assemble(tile, cycle_data):
    side = tile.shape[0]
    wide = side + 6
    channels = tile.shape[-1]
    band = 3 * wide
    top = cycle_data[:band].reshape(3, wide, channels)
    middle = cycle_data[band : band + 6 * side].reshape(side, 6, channels)
    bottom = cycle_data[band + 6 * side :].reshape(3, wide, channels)
    centre = jnp.concatenate([middle[:, :3], tile, middle[:, 3:]], axis=1)
    return jnp.concatenate([top, centre, bottom], axis=0)


def ring_of(square, side):
    channels = square.shape[-1]
    top = square[:3].reshape(-1, channels)
    middle = jnp.concatenate([square[3 : side + 3, :3], square[3 : side + 3, side + 3 :]], axis=1)
    bottom = square[side + 3 :].reshape(-1, channels)
    return jnp.concatenate([top, middle.reshape(-1, channels), bottom], axis=0)


def shifted_conv(square, kern, out_side):
    total = None
    for di in range(7):
        for dj in range(7):
            term = square[di : di + out_side, dj : dj + out_side] * kern[di, dj]
            total = term if total is None else total + term
    return total


def tap_sums(square, d_square, side):
    return jnp.stack(
        [
            jnp.sum(square[di : di + side, dj : dj + side] * d_square, axis=(0, 1))
            for di in range(7)
            for dj in range(7)
        ]
    )


def normal_cdf(values):
    return 0.5 * (1.0 + lax.erf(values * 0.7071067811865476))


def move_round(blocks, heading, axis):
    along = 0 if axis == "face" else 1
    moved = list(blocks[k] for k in range(len(LINK_OFFSETS)))
    for sign in (-1, 1):
        group = [k for k, offset in enumerate(LINK_OFFSETS) if offset[along] == sign]
        shifted = from_behind(jnp.stack([moved[k] for k in group]), axis, sign * heading)
        for place, k in enumerate(group):
            moved[k] = shifted[place]
    return jnp.stack(moved)


def move_links(blocks, heading):
    return move_round(move_round(blocks, heading, "face"), heading, "tile")


def local(
    loader,
    row_tile,
    row_pixel,
    neighbours,
    send_pixels,
    halo_from,
    cotangent,
    kernel,
    conv_bias,
    norm_gain,
    norm_bias,
    weight_in,
    bias_in,
    weight_out,
    bias_out,
    layer_scale,
):
    grid_rows = lax.axis_size("face")
    grid_cols = lax.axis_size("tile")
    tile_count = grid_rows * grid_cols
    pixel_count = loader.shape[1]
    channels = loader.shape[2]
    capacity = send_pixels.shape[2]
    per_peer = pixel_count // tile_count
    tile_side = math.isqrt(pixel_count)
    cycle_rows, cycle_cols = cycle_cells(tile_side)
    factor = 1.0 / math.sqrt(lax.axis_size("dp") * tile_count * pixel_count)
    _, ordering, sorted_pixels = lax.sort(
        (row_tile, jnp.arange(row_tile.shape[0], dtype=jnp.int32), row_pixel), num_keys=1, is_stable=True
    )
    outgoing = loader[0][ordering].reshape(tile_count, per_peer, channels)
    labels = sorted_pixels.reshape(tile_count, per_peer)
    digits = jnp.concatenate([labels // 32, labels % 32], axis=1).astype(loader.dtype)
    label_row = jnp.pad(digits, ((0, 0), (0, channels - 2 * per_peer)))[:, None, :]
    parcel = lax.all_to_all(
        jnp.concatenate([outgoing, label_row], axis=1),
        ("face", "tile"),
        split_axis=0,
        concat_axis=0,
        tiled=True,
    )
    arrived = parcel[:, :per_peer]
    got = parcel[:, per_peer, : 2 * per_peer].astype(jnp.int32)
    places = got[:, :per_peer] * 32 + got[:, per_peer:]
    field = (
        jnp.zeros((pixel_count, channels), loader.dtype)
        .at[places.reshape(-1)]
        .set(arrived.reshape(-1, channels))
    )
    my_row = lax.axis_index("face")
    my_col = lax.axis_index("tile")
    row_steps = jnp.asarray([offset[0] for offset in LINK_OFFSETS], jnp.int32)
    col_steps = jnp.asarray([offset[1] for offset in LINK_OFFSETS], jnp.int32)
    sources = (my_row - row_steps) % grid_rows * grid_cols + (my_col - col_steps) % grid_cols
    senders = halo_from[0] // capacity
    matching = senders[:, None] == sources[None, :]
    link_of = jnp.sum(matching.astype(jnp.int32) * jnp.arange(8, dtype=jnp.int32)[None, :], axis=1)
    readable = jnp.any(matching, axis=1)
    recv_index = jnp.where(readable, link_of * capacity + halo_from[0] % capacity, 8 * capacity)
    live = (neighbours[0] < tile_count)[:, None, None]
    extended = jnp.concatenate([field, jnp.zeros((1, channels), field.dtype)], axis=0)
    blocks_out = jnp.where(live, extended[send_pixels[0]], jnp.zeros((), field.dtype))
    received = move_links(blocks_out, 1)
    flat_recv = jnp.concatenate(
        [received.reshape(8 * capacity, channels), jnp.zeros((1, channels), field.dtype)], axis=0
    )
    cycle_data = flat_recv[recv_index]
    padded = assemble(field.reshape(tile_side, tile_side, channels), cycle_data)
    kern_f = kernel.astype(jnp.float32).reshape(7, 7, channels)
    padded_f = padded.astype(jnp.float32)
    mixed = shifted_conv(padded_f, kern_f, tile_side).reshape(pixel_count, channels) + conv_bias
    average = jnp.mean(mixed, axis=-1, keepdims=True)
    centred = mixed - average
    inv_scale = lax.rsqrt(jnp.mean(centred * centred, axis=-1, keepdims=True) + 1e-06)
    standard = centred * inv_scale
    normed = (standard * norm_gain + norm_bias).astype(jnp.bfloat16)
    hidden = jnp.dot(normed, weight_in, preferred_element_type=jnp.float32) + bias_in
    cdf_vals = normal_cdf(hidden)
    active = (hidden * cdf_vals).astype(jnp.bfloat16)
    branch = jnp.dot(active, weight_out, preferred_element_type=jnp.float32) + bias_out
    block_out = (field.astype(jnp.float32) + layer_scale * branch).astype(jnp.bfloat16)
    grad_f = cotangent[0].astype(jnp.float32)
    g_scale = jnp.sum(grad_f * branch, axis=0) * factor
    d_branch = (grad_f * layer_scale).astype(jnp.bfloat16)
    g_w_out = jnp.dot(active.T, d_branch, preferred_element_type=jnp.float32) * factor
    g_b_out = jnp.sum(d_branch.astype(jnp.float32), axis=0) * factor
    d_active = jnp.dot(d_branch, weight_out.T, preferred_element_type=jnp.float32)
    slope = cdf_vals + hidden * jnp.exp(-0.5 * hidden * hidden) * 0.3989422804014327
    d_hidden = (d_active * slope).astype(jnp.bfloat16)
    g_w_in = jnp.dot(normed.T, d_hidden, preferred_element_type=jnp.float32) * factor
    g_b_in = jnp.sum(d_hidden.astype(jnp.float32), axis=0) * factor
    d_normed = jnp.dot(d_hidden, weight_in.T, preferred_element_type=jnp.float32)
    g_gain = jnp.sum(d_normed * standard, axis=0) * factor
    g_nbias = jnp.sum(d_normed, axis=0) * factor
    scaled = d_normed * norm_gain
    d_mixed = (
        inv_scale
        * (
            scaled
            - jnp.mean(scaled, axis=-1, keepdims=True)
            - standard * jnp.mean(scaled * standard, axis=-1, keepdims=True)
        )
    ).astype(jnp.bfloat16)
    g_cbias = jnp.sum(d_mixed.astype(jnp.float32), axis=0) * factor
    d_square = d_mixed.astype(jnp.float32).reshape(tile_side, tile_side, channels)
    d_pad = shifted_conv(
        jnp.pad(d_square, ((6, 6), (6, 6), (0, 0))), kern_f[::-1, ::-1], tile_side + 6
    )
    g_kern = tap_sums(padded_f, d_square, tile_side) * factor
    inner_grad = d_pad[3 : tile_side + 3, 3 : tile_side + 3].reshape(pixel_count, channels)
    cycle_grad = ring_of(d_pad, tile_side).astype(jnp.bfloat16)
    back_parcel = (
        jnp.zeros((8 * capacity + 1, channels), jnp.bfloat16).at[recv_index].set(cycle_grad)
    )
    back_parcel = back_parcel[: 8 * capacity].reshape(8, capacity, channels)

    def finish(moved):
        returned = jnp.where(live, moved, jnp.zeros((), moved.dtype))
        incoming = (
            jnp.zeros((pixel_count + 1, channels), jnp.float32)
            .at[send_pixels[0].reshape(-1)]
            .add(returned.reshape(-1, channels).astype(jnp.float32))
        )
        return (grad_f + inner_grad + incoming[:pixel_count]).astype(jnp.bfloat16)

    sums, field_grad = tree_sum(
        (g_kern, g_cbias, g_gain, g_nbias, g_w_in, g_b_in, g_w_out, g_b_out, g_scale),
        ("dp", "tile"),
        ("face",),
        rider=back_parcel,
        stages=(
            (1, lambda parcel: move_round(parcel, -1, "face")),
            (3, lambda parcel: move_round(parcel, -1, "tile")),
            (5, finish),
        ),
    )
    g_kern, g_cbias, g_gain, g_nbias, g_w_in, g_b_in, g_w_out, g_b_out, g_scale = sums
    return (
        block_out[None],
        field_grad[None],
        g_kern,
        g_cbias,
        g_gain,
        g_nbias,
        g_w_in,
        g_b_in,
        g_w_out,
        g_b_out,
        g_scale,
    )


def solution(mesh):
    placed = (
        P("dp", ("face", "tile"), None),
        P(("face", "tile")),
        P(("face", "tile")),
        P(("face", "tile"), None),
        P(("face", "tile"), None, None),
        P(("face", "tile"), None),
        P("dp", ("face", "tile"), None),
        P(),
        P(),
        P(),
        P(),
        P(),
        P(),
        P(),
        P(),
        P(),
    )
    return jax.shard_map(
        local,
        mesh=mesh,
        in_specs=placed,
        out_specs=(
            P("dp", ("face", "tile"), None),
            P("dp", ("face", "tile"), None),
            P(),
            P(),
            P(),
            P(),
            P(),
            P(),
            P(),
            P(),
            P(),
        ),
        check_vma=False,
    )
```

```python
import math

import jax
import jax.numpy as jnp
import numpy as np
from jax import lax
from jax.sharding import PartitionSpec as P

LINK_OFFSETS = ((-1, -1), (-1, 0), (-1, 1), (0, -1), (0, 1), (1, -1), (1, 0), (1, 1))


def from_behind(value, axis, steps):
    count = lax.axis_size(axis)
    pairs = [(source, (source + steps) % count) for source in range(count)]
    return lax.ppermute(value, axis, pairs)


def tree_sum(parts, halving_axes, doubling_axes, rider=None, stages=()):
    flat = jnp.concatenate([part.reshape(-1) for part in parts])

    def bits_of(axes):
        steps = []
        for axis in axes:
            size = lax.axis_size(axis)
            bit = 1
            while bit < size:
                steps.append((axis, bit, size))
                bit *= 2
        return steps

    halving = bits_of(halving_axes)
    plan = dict(stages)
    count = [0]

    def stepped(buf):
        nonlocal rider
        count[0] += 1
        if count[0] in plan:
            buf, rider = lax.optimization_barrier((buf, rider))
            rider = plan[count[0]](rider)
        return buf

    total = flat.shape[0]
    pad = (-total) % (1 << len(halving))
    buf = jnp.pad(flat, (0, pad))
    for axis in halving_axes:
        size = lax.axis_size(axis)
        digit = lax.axis_index(axis)
        chunks = jnp.split(buf, size)

        def chunk_at(index):
            chosen = chunks[size - 1]
            for place in reversed(range(size - 1)):
                chosen = jnp.where(index == place, chunks[place], chosen)
            return chosen

        total_chunk = chunk_at(digit)
        for flip in range(1, size):
            pairs = [(i, i ^ flip) for i in range(size)]
            total_chunk = total_chunk + lax.ppermute(chunk_at(digit ^ flip), axis, pairs)
        buf = stepped(total_chunk)
    for axis, bit, size in bits_of(doubling_axes):
        buf = stepped(buf + lax.ppermute(buf, axis, [(i, i ^ bit) for i in range(size)]))
    for axis in reversed(halving_axes):
        size = lax.axis_size(axis)
        digit = lax.axis_index(axis)
        pieces = [buf] + [
            lax.ppermute(buf, axis, [(i, i ^ flip) for i in range(size)]) for flip in range(1, size)
        ]
        placed = []
        for place in range(size):
            source = place ^ digit
            chosen = pieces[size - 1]
            for flip in reversed(range(size - 1)):
                chosen = jnp.where(source == flip, pieces[flip], chosen)
            placed.append(chosen)
        buf = stepped(jnp.concatenate(placed))
    out = []
    start = 0
    for part in parts:
        out.append(buf[start : start + part.size].reshape(part.shape))
        start += part.size
    return tuple(out), rider

def cycle_cells(tile_side):
    padded_side = tile_side + 6
    cell_rows, cell_cols = np.meshgrid(
        np.arange(padded_side), np.arange(padded_side), indexing="ij"
    )
    inside = (
        (cell_rows >= 3)
        & (cell_rows < tile_side + 3)
        & (cell_cols >= 3)
        & (cell_cols < tile_side + 3)
    )
    outside = (~inside).reshape(-1)
    return (cell_rows.reshape(-1)[outside], cell_cols.reshape(-1)[outside])


def depthwise(field_in, kern_in):
    return lax.conv_general_dilated(
        field_in,
        kern_in,
        (1, 1),
        "VALID",
        dimension_numbers=("NHWC", "HWIO", "NHWC"),
        feature_group_count=field_in.shape[-1],
        precision=lax.Precision.HIGHEST,
    )


def assemble(tile, cycle_data):
    side = tile.shape[0]
    wide = side + 6
    channels = tile.shape[-1]
    band = 3 * wide
    top = cycle_data[:band].reshape(3, wide, channels)
    middle = cycle_data[band : band + 6 * side].reshape(side, 6, channels)
    bottom = cycle_data[band + 6 * side :].reshape(3, wide, channels)
    centre = jnp.concatenate([middle[:, :3], tile, middle[:, 3:]], axis=1)
    return jnp.concatenate([top, centre, bottom], axis=0)


def ring_of(square, side):
    channels = square.shape[-1]
    top = square[:3].reshape(-1, channels)
    middle = jnp.concatenate([square[3 : side + 3, :3], square[3 : side + 3, side + 3 :]], axis=1)
    bottom = square[side + 3 :].reshape(-1, channels)
    return jnp.concatenate([top, middle.reshape(-1, channels), bottom], axis=0)


def shifted_conv(square, kern, out_side):
    total = None
    for di in range(7):
        for dj in range(7):
            term = square[di : di + out_side, dj : dj + out_side] * kern[di, dj]
            total = term if total is None else total + term
    return total


def tap_sums(square, d_square, side):
    return jnp.stack(
        [
            jnp.sum(square[di : di + side, dj : dj + side] * d_square, axis=(0, 1))
            for di in range(7)
            for dj in range(7)
        ]
    )


def normal_cdf(values):
    return 0.5 * (1.0 + lax.erf(values * 0.7071067811865476))


def move_round(blocks, heading, axis):
    along = 0 if axis == "face" else 1
    moved = list(blocks[k] for k in range(len(LINK_OFFSETS)))
    for sign in (-1, 1):
        group = [k for k, offset in enumerate(LINK_OFFSETS) if offset[along] == sign]
        shifted = from_behind(jnp.stack([moved[k] for k in group]), axis, sign * heading)
        for place, k in enumerate(group):
            moved[k] = shifted[place]
    return jnp.stack(moved)


def move_links(blocks, heading):
    return move_round(move_round(blocks, heading, "face"), heading, "tile")


def local(
    loader,
    row_tile,
    row_pixel,
    neighbours,
    send_pixels,
    halo_from,
    cotangent,
    kernel,
    conv_bias,
    norm_gain,
    norm_bias,
    weight_in,
    bias_in,
    weight_out,
    bias_out,
    layer_scale,
):
    grid_rows = lax.axis_size("face")
    grid_cols = lax.axis_size("tile")
    tile_count = grid_rows * grid_cols
    pixel_count = loader.shape[1]
    channels = loader.shape[2]
    capacity = send_pixels.shape[2]
    per_peer = pixel_count // tile_count
    tile_side = math.isqrt(pixel_count)
    cycle_rows, cycle_cols = cycle_cells(tile_side)
    factor = 1.0 / math.sqrt(lax.axis_size("dp") * tile_count * pixel_count)
    _, ordering, sorted_pixels = lax.sort(
        (row_tile, jnp.arange(row_tile.shape[0], dtype=jnp.int32), row_pixel), num_keys=1, is_stable=True
    )
    outgoing = loader[0][ordering].reshape(tile_count, per_peer, channels)
    labels = sorted_pixels.reshape(tile_count, per_peer)
    digits = jnp.concatenate([labels // 32, labels % 32], axis=1).astype(loader.dtype)
    label_row = jnp.pad(digits, ((0, 0), (0, channels - 2 * per_peer)))[:, None, :]
    parcel = lax.all_to_all(
        jnp.concatenate([outgoing, label_row], axis=1),
        ("face", "tile"),
        split_axis=0,
        concat_axis=0,
        tiled=True,
    )
    arrived = parcel[:, :per_peer]
    got = parcel[:, per_peer, : 2 * per_peer].astype(jnp.int32)
    places = got[:, :per_peer] * 32 + got[:, per_peer:]
    field = (
        jnp.zeros((pixel_count, channels), loader.dtype)
        .at[places.reshape(-1)]
        .set(arrived.reshape(-1, channels))
    )
    my_row = lax.axis_index("face")
    my_col = lax.axis_index("tile")
    row_steps = jnp.asarray([offset[0] for offset in LINK_OFFSETS], jnp.int32)
    col_steps = jnp.asarray([offset[1] for offset in LINK_OFFSETS], jnp.int32)
    sources = (my_row - row_steps) % grid_rows * grid_cols + (my_col - col_steps) % grid_cols
    senders = halo_from[0] // capacity
    matching = senders[:, None] == sources[None, :]
    link_of = jnp.sum(matching.astype(jnp.int32) * jnp.arange(8, dtype=jnp.int32)[None, :], axis=1)
    readable = jnp.any(matching, axis=1)
    recv_index = jnp.where(readable, link_of * capacity + halo_from[0] % capacity, 8 * capacity)
    live = (neighbours[0] < tile_count)[:, None, None]
    extended = jnp.concatenate([field, jnp.zeros((1, channels), field.dtype)], axis=0)
    blocks_out = jnp.where(live, extended[send_pixels[0]], jnp.zeros((), field.dtype))
    received = move_links(blocks_out, 1)
    flat_recv = jnp.concatenate(
        [received.reshape(8 * capacity, channels), jnp.zeros((1, channels), field.dtype)], axis=0
    )
    cycle_data = flat_recv[recv_index]
    padded = assemble(field.reshape(tile_side, tile_side, channels), cycle_data)
    kern_f = kernel.astype(jnp.float32).reshape(7, 7, channels)
    padded_f = padded.astype(jnp.float32)
    mixed = shifted_conv(padded_f, kern_f, tile_side).reshape(pixel_count, channels) + conv_bias
    average = jnp.mean(mixed, axis=-1, keepdims=True)
    centred = mixed - average
    inv_scale = lax.rsqrt(jnp.mean(centred * centred, axis=-1, keepdims=True) + 1e-06)
    standard = centred * inv_scale
    normed = (standard * norm_gain + norm_bias).astype(jnp.bfloat16)
    hidden = jnp.dot(normed, weight_in, preferred_element_type=jnp.float32) + bias_in
    cdf_vals = normal_cdf(hidden)
    active = (hidden * cdf_vals).astype(jnp.bfloat16)
    branch = jnp.dot(active, weight_out, preferred_element_type=jnp.float32) + bias_out
    block_out = (field.astype(jnp.float32) + layer_scale * branch).astype(jnp.bfloat16)
    grad_f = cotangent[0].astype(jnp.float32)
    g_scale = jnp.sum(grad_f * branch, axis=0) * factor
    d_branch = (grad_f * layer_scale).astype(jnp.bfloat16)
    g_w_out = jnp.dot(active.T, d_branch, preferred_element_type=jnp.float32) * factor
    g_b_out = jnp.sum(d_branch.astype(jnp.float32), axis=0) * factor
    d_active = jnp.dot(d_branch, weight_out.T, preferred_element_type=jnp.float32)
    slope = cdf_vals + hidden * jnp.exp(-0.5 * hidden * hidden) * 0.3989422804014327
    d_hidden = (d_active * slope).astype(jnp.bfloat16)
    g_w_in = jnp.dot(normed.T, d_hidden, preferred_element_type=jnp.float32) * factor
    g_b_in = jnp.sum(d_hidden.astype(jnp.float32), axis=0) * factor
    d_normed = jnp.dot(d_hidden, weight_in.T, preferred_element_type=jnp.float32)
    g_gain = jnp.sum(d_normed * standard, axis=0) * factor
    g_nbias = jnp.sum(d_normed, axis=0) * factor
    scaled = d_normed * norm_gain
    d_mixed = (
        inv_scale
        * (
            scaled
            - jnp.mean(scaled, axis=-1, keepdims=True)
            - standard * jnp.mean(scaled * standard, axis=-1, keepdims=True)
        )
    ).astype(jnp.bfloat16)
    g_cbias = jnp.sum(d_mixed.astype(jnp.float32), axis=0) * factor
    d_square = d_mixed.astype(jnp.float32).reshape(tile_side, tile_side, channels)
    d_pad = shifted_conv(
        jnp.pad(d_square, ((6, 6), (6, 6), (0, 0))), kern_f[::-1, ::-1], tile_side + 6
    )
    g_kern = tap_sums(padded_f, d_square, tile_side) * factor
    inner_grad = d_pad[3 : tile_side + 3, 3 : tile_side + 3].reshape(pixel_count, channels)
    cycle_grad = ring_of(d_pad, tile_side).astype(jnp.bfloat16)
    back_parcel = (
        jnp.zeros((8 * capacity + 1, channels), jnp.bfloat16).at[recv_index].set(cycle_grad)
    )
    back_parcel = back_parcel[: 8 * capacity].reshape(8, capacity, channels)

    def finish(moved):
        returned = jnp.where(live, moved, jnp.zeros((), moved.dtype))
        spread = (
            jnp.arange(pixel_count + 1, dtype=jnp.int32)[:, None] == send_pixels[0].reshape(1, -1)
        ).astype(returned.dtype)
        incoming = jnp.dot(
            spread, returned.reshape(-1, channels), preferred_element_type=jnp.float32
        )
        return (grad_f + inner_grad + incoming[:pixel_count]).astype(jnp.bfloat16)

    sums, field_grad = tree_sum(
        (g_kern, g_cbias, g_gain, g_nbias, g_w_in, g_b_in, g_w_out, g_b_out, g_scale),
        ("dp", "tile"),
        ("face",),
        rider=back_parcel,
        stages=(
            (1, lambda parcel: move_round(parcel, -1, "face")),
            (3, lambda parcel: move_round(parcel, -1, "tile")),
            (5, finish),
        ),
    )
    g_kern, g_cbias, g_gain, g_nbias, g_w_in, g_b_in, g_w_out, g_b_out, g_scale = sums
    return (
        block_out[None],
        field_grad[None],
        g_kern,
        g_cbias,
        g_gain,
        g_nbias,
        g_w_in,
        g_b_in,
        g_w_out,
        g_b_out,
        g_scale,
    )


def solution(mesh):
    placed = (
        P("dp", ("face", "tile"), None),
        P(("face", "tile")),
        P(("face", "tile")),
        P(("face", "tile"), None),
        P(("face", "tile"), None, None),
        P(("face", "tile"), None),
        P("dp", ("face", "tile"), None),
        P(),
        P(),
        P(),
        P(),
        P(),
        P(),
        P(),
        P(),
        P(),
    )
    return jax.shard_map(
        local,
        mesh=mesh,
        in_specs=placed,
        out_specs=(
            P("dp", ("face", "tile"), None),
            P("dp", ("face", "tile"), None),
            P(),
            P(),
            P(),
            P(),
            P(),
            P(),
            P(),
            P(),
            P(),
        ),
        check_vma=False,
    )
```
